256 devices in a mesh: rows: 32 (over z, x), rep: 8 (over y, core).
Axes of the slice: x: 4, y: 4, z: 8, core: 2. Of those that a mesh axis runs over, the one named last changes fastest.
Arguments:
- grad_shards: bfloat16 [8, 3, 2048, 2048], P('rep', None, 'rows'), may hold values from -6 to 6
- error_shards: float32 [8, 3, 2048, 2048], P('rep', None, 'rows'), may hold values from -4 to 4
- momentum: float32 [3, 2048, 2048], P(None, 'rows'), may hold values from -6 to 6
- weights: float32 [3, 2048, 2048], P(None, 'rows'), may hold values from -0.125 to 0.125
- q_start: float32 [3, 2048, 32], replicated, may hold values from -6 to 6
- vec_grads: float32 [8, 16, 2048], P('rep', None, 'rows'), may hold values from -6 to 6
- vec_momentum: float32 [16, 2048], P(None, 'rows'), may hold values from -6 to 6
- vec_weights: float32 [16, 2048], P(None, 'rows'), may hold values from -1 to 1
Outputs:
- new_errors: float32 [8, 3, 2048, 2048], P('rep', None, 'rows')
- new_momentum: float32 [3, 2048, 2048], P(None, 'rows')
- new_weights: float32 [3, 2048, 2048], P(None, 'rows')
- new_vec_momentum: float32 [16, 2048], P(None, 'rows')
- new_vec_weights: float32 [16, 2048], P(None, 'rows')
The draws below stay inside these ranges and needn't reach their ends.
All inputs are finite; a program needn't handle non-finite values.
Results may differ from the reference program's by a relative error of at most 0.0003.
Values sent between devices are 32-bit elements; how exact they have to be, the bound alone decides.
No kernel may reach another device: no remote copies, remote signals or barrier semaphores. Data moves between devices by JAX's collectives and lax.ppermute only.
A program may use at most 64 MiB of HBM per device.

```python
import jax
import jax.numpy as jnp
from jax import lax

D = 2048
RANK = 32
MATS = 3
ROUNDS = 2
NVEC = 16
N_REP = 8


def block_levels(stream_key, dims, shards, low, high):
    level, own = 1.0, jax.random.fold_in(stream_key, 6)
    for position, blocks in shards:
        heights = jnp.exp(jax.random.uniform(jax.random.fold_in(own, position), (blocks,), jnp.float32, low / len(shards), high / len(shards)))
        level = level * jnp.repeat(heights, dims[position] // blocks).reshape([-1 if axis == position else 1 for axis in range(len(dims))])
    return level


def bell_draw(stream_key, shape, scale, bound, split=(), kind=jnp.bfloat16):
    factor_of = block_levels(stream_key, shape, split, -0.22, 0.18) if split else 1.0
    array = jax.random.normal(stream_key, shape, jnp.float32) * scale * factor_of
    return jnp.minimum(jnp.maximum(array, -bound), bound).astype(kind)


def setup_inputs(seed: int = 0) -> dict:
    arg_keys = jax.random.split(jax.random.key(seed), 9)
    return {
        "grad_shards": bell_draw(arg_keys[0], (N_REP, MATS, D, D), 1.0, 6.0, ((0, 8), (2, 32))),
        "error_shards": bell_draw(arg_keys[1], (N_REP, MATS, D, D), 0.3, 4.0, ((0, 8), (2, 32)), jnp.float32),
        "momentum": bell_draw(arg_keys[2], (MATS, D, D), 0.5, 6.0, ((1, 32),), jnp.float32),
        "weights": bell_draw(arg_keys[3], (MATS, D, D), D ** -0.5, 0.125, ((1, 32),), jnp.float32),
        "q_start": bell_draw(arg_keys[4], (MATS, D, RANK), 1.0, 6.0, (), jnp.float32),
        "vec_grads": bell_draw(arg_keys[5], (N_REP, NVEC, D), 1.0, 6.0, ((0, 8), (2, 32)), jnp.float32),
        "vec_momentum": bell_draw(arg_keys[6], (NVEC, D), 0.5, 6.0, ((1, 32),), jnp.float32),
        "vec_weights": jnp.clip(jax.random.uniform(arg_keys[7], (NVEC, D), jnp.float32, -1.0, 1.0) * block_levels(arg_keys[7], (NVEC, D), ((1, 32),), -0.4, 0.0), -1.0, 1.0),
    }


learn_rate = 0.1
momentum_beta = 0.9

def orthonormal(factor_p):
    gram_mat = jnp.einsum('mrk,mrl->mkl', factor_p, factor_p, precision=lax.Precision.HIGHEST)
    factor_l = jnp.linalg.cholesky(gram_mat)
    solved = lax.linalg.triangular_solve(factor_l, jnp.swapaxes(factor_p, 1, 2), left_side=True, lower=True)
    return jnp.swapaxes(solved, 1, 2)

def reference(grad_shards, error_shards, momentum, weights, q_start, vec_grads, vec_momentum, vec_weights):
    merged = grad_shards.astype(jnp.float32) + error_shards
    factor_q = q_start
    ortho_p = None
    for repeat in range(ROUNDS):
        factor_p = jnp.einsum('nmrd,mdk->mrk', merged, factor_q, precision=lax.Precision.HIGHEST)
        ortho_p = orthonormal(factor_p)
        factor_q = jnp.einsum('nmrd,mrk->mdk', merged, ortho_p, precision=lax.Precision.HIGHEST)
    low_rank = jnp.einsum('mrk,mdk->mrd', ortho_p, factor_q / N_REP, precision=lax.Precision.HIGHEST)
    new_errors = merged - low_rank[None]
    new_momentum = momentum_beta * momentum + low_rank
    new_weights = weights - learn_rate * new_momentum
    vec_mean = jnp.sum(vec_grads, axis=0) / N_REP
    new_vec_momentum = momentum_beta * vec_momentum + vec_mean
    new_vec_weights = vec_weights - learn_rate * new_vec_momentum
    return (new_errors, new_momentum, new_weights, new_vec_momentum, new_vec_weights)
```

```python
import jax
import jax.numpy as jnp
import numpy as np
from jax import lax
from jax.sharding import Mesh
from jax.sharding import PartitionSpec as P

ROUNDS = 2

learn_rate = 0.1
momentum_beta = 0.9


OUTER_ROWS, INNER_ROWS, OUTER_REP, INNER_REP = "zr", "xr", "yr", "cr"
ALL = (OUTER_ROWS, INNER_ROWS, OUTER_REP, INNER_REP)
REP = (OUTER_REP, INNER_REP)


def _sub_mesh(mesh):
    rows, rep = mesh.shape["rows"], mesh.shape["rep"]
    devs = np.asarray(mesh.devices)
    xs = []
    for d in devs[:, 0]:
        c = getattr(d, "coords", None)
        if c is None:
            break
        c = tuple(c)
        if xs and c[1:] != xs[0][1:]:
            break
        xs.append(c)
    inner_rows = len(xs) if xs and rows % len(xs) == 0 else 1
    inner_rep = 2 if rep % 2 == 0 else 1
    shape = (rows // inner_rows, inner_rows, rep // inner_rep, inner_rep)
    return Mesh(devs.reshape(shape), ALL)


def _shift(v, axis, s, n):
    return lax.ppermute(v, axis, [(i, (i + s) % n) for i in range(n)])


def _rs(b, axis, n):
    if n == 1:
        return b
    size = b.shape[0] // n
    k = lax.axis_index(axis)
    acc = lax.dynamic_slice_in_dim(b, k * size, size, 0)
    for s in range(1, n):
        part = lax.dynamic_slice_in_dim(b, ((k + s) % n) * size, size, 0)
        acc = acc + _shift(part, axis, s, n)
    return acc


def _ag(c, axis, n):
    if n == 1:
        return c
    size = c.shape[0]
    k = lax.axis_index(axis)
    out = jnp.zeros((n * size,) + c.shape[1:], c.dtype)
    out = lax.dynamic_update_slice_in_dim(out, c, k * size, 0)
    for s in range(1, n):
        out = lax.dynamic_update_slice_in_dim(out, _shift(c, axis, s, n), ((k - s) % n) * size, 0)
    return out


def _ar_direct(c, axis, n):
    if n == 1:
        return c
    k = lax.axis_index(axis)
    vals = jnp.stack([c] + [_shift(c, axis, s, n) for s in range(1, n)])
    ordered = jnp.take(vals, (k - jnp.arange(n)) % n, axis=0)
    return jnp.sum(ordered, axis=0)


def solution(mesh):
    sub = _sub_mesh(mesh)
    nz, nx, ny, nc = (sub.shape[a] for a in ALL)

    def ar_rep(b):
        return _ar_direct(_ar_direct(b, INNER_REP, nc), OUTER_REP, ny)

    def ar_all(b):
        b = _rs(_rs(b, INNER_REP, nc), OUTER_REP, ny)
        b = _ar_direct(b, INNER_ROWS, nx)
        b = _ag(_rs(b, OUTER_ROWS, nz), OUTER_ROWS, nz)
        return _ag(_ag(b, OUTER_REP, ny), INNER_REP, nc)

    def shards(
        grad_shards, error_shards, momentum, weights, q_start, vec_grads, vec_momentum, vec_weights
    ):
        replicas = lax.axis_size(OUTER_REP) * lax.axis_size(INNER_REP)
        first_rep = (lax.axis_index(OUTER_REP) == 0) & (lax.axis_index(INNER_REP) == 0)
        mats, rows, width = grad_shards.shape[1:]
        rank = q_start.shape[2]
        merged = grad_shards[0].astype(jnp.float32) + error_shards[0]
        factor_qt = jnp.swapaxes(q_start, 1, 2)
        vec = vec_grads[0]
        vec_sum = None
        ortho_pt = None
        lanes = 128
        group = lanes * nz * nx * ny * nc
        for repeat in range(ROUNDS):
            local_pt = jnp.einsum("mrd,mkd->mkr", merged, factor_qt, precision=lax.Precision.HIGHEST)
            flat_p = local_pt.reshape(-1)
            if repeat == 0:
                flat = jnp.concatenate([flat_p, vec.reshape(-1)])
                summed = ar_rep(flat.reshape(-1, rows)).reshape(-1)
                vec_sum = summed[flat_p.size :].reshape(vec.shape)
                summed_pt = summed[: flat_p.size].reshape(local_pt.shape)
            else:
                summed_pt = ar_rep(local_pt.reshape(-1, rows)).reshape(local_pt.shape)
            local_gram = jnp.einsum("mkr,mlr->mkl", summed_pt, summed_pt, precision=lax.Precision.HIGHEST)
            local_gram = jnp.where(first_rep, local_gram, jnp.zeros_like(local_gram))
            local_qt = jnp.einsum("mrd,mkr->mkd", merged, summed_pt, precision=lax.Precision.HIGHEST)
            pieces = [local_qt.reshape(-1), local_gram.reshape(-1)]
            used = sum(x.size for x in pieces)
            padded = -(-used // group) * group
            pieces.append(jnp.zeros((padded - used,), jnp.float32))
            packed = jnp.concatenate(pieces).reshape(-1, lanes)
            total = ar_all(packed).reshape(-1)
            qt_un = total[: local_qt.size].reshape(local_qt.shape)
            gram_mat = total[local_qt.size : used].reshape(local_gram.shape)
            factor_l = jnp.linalg.cholesky(gram_mat)
            if repeat == ROUNDS - 1:
                rhs = jnp.concatenate([summed_pt, qt_un], axis=2)
                solved = lax.linalg.triangular_solve(factor_l, rhs, left_side=True, lower=True)
                ortho_pt = solved[:, :, :rows]
                factor_qt = solved[:, :, rows:]
            else:
                factor_qt = lax.linalg.triangular_solve(factor_l, qt_un, left_side=True, lower=True)
        low_rank = jnp.einsum(
            "mkr,mkd->mrd", ortho_pt, factor_qt / replicas, precision=lax.Precision.HIGHEST
        )
        new_errors = (merged - low_rank)[None]
        new_momentum = momentum_beta * momentum + low_rank
        new_weights = weights - learn_rate * new_momentum
        vec_mean = vec_sum / replicas
        new_vec_momentum = momentum_beta * vec_momentum + vec_mean
        new_vec_weights = vec_weights - learn_rate * new_vec_momentum
        return (new_errors, new_momentum, new_weights, new_vec_momentum, new_vec_weights)

    rows_axes = (OUTER_ROWS, INNER_ROWS)
    rep_axes = REP
    return jax.shard_map(
        shards,
        mesh=sub,
        in_specs=(
            P(rep_axes, None, rows_axes, None),
            P(rep_axes, None, rows_axes, None),
            P(None, rows_axes, None),
            P(None, rows_axes, None),
            P(),
            P(rep_axes, None, rows_axes),
            P(None, rows_axes),
            P(None, rows_axes),
        ),
        out_specs=(
            P(rep_axes, None, rows_axes, None),
            P(None, rows_axes, None),
            P(None, rows_axes, None),
            P(None, rows_axes),
            P(None, rows_axes),
        ),
        check_vma=False,
    )
```

```python
import jax
import jax.numpy as jnp
import numpy as np
from jax import lax
from jax.sharding import Mesh
from jax.sharding import PartitionSpec as P

ROUNDS = 2

learn_rate = 0.1
momentum_beta = 0.9


OUTER_ROWS, INNER_ROWS, OUTER_REP, INNER_REP = "zr", "xr", "yr", "cr"
ALL = (OUTER_ROWS, INNER_ROWS, OUTER_REP, INNER_REP)
REP = (OUTER_REP, INNER_REP)


def _sub_mesh(mesh):
    rows, rep = mesh.shape["rows"], mesh.shape["rep"]
    devs = np.asarray(mesh.devices)
    xs = []
    for d in devs[:, 0]:
        c = getattr(d, "coords", None)
        if c is None:
            break
        c = tuple(c)
        if xs and c[1:] != xs[0][1:]:
            break
        xs.append(c)
    inner_rows = len(xs) if xs and rows % len(xs) == 0 else 1
    inner_rep = 2 if rep % 2 == 0 else 1
    shape = (rows // inner_rows, inner_rows, rep // inner_rep, inner_rep)
    return Mesh(devs.reshape(shape), ALL)


def _xor(v, axis, d, n):
    return lax.ppermute(v, axis, [(i, i ^ d) for i in range(n)])


def _halves(n):
    d = n // 2
    while d >= 1:
        yield d
        d //= 2


def _bfly(c, axis, n):
    d = 1
    while d < n:
        c = c + _xor(c, axis, d, n)
        d *= 2
    return c


def _rs(b, axis, n):
    k = lax.axis_index(axis)
    for d in _halves(n):
        half = b.shape[0] // 2
        bit = (k // d) % 2
        keep = lax.dynamic_slice_in_dim(b, bit * half, half, 0)
        send = lax.dynamic_slice_in_dim(b, (1 - bit) * half, half, 0)
        b = keep + _xor(send, axis, d, n)
    return b


def _ag(c, axis, n):
    k = lax.axis_index(axis)
    d = 1
    while d < n:
        recv = _xor(c, axis, d, n)
        upper = (k // d) % 2 == 1
        c = jnp.concatenate([jnp.where(upper, recv, c), jnp.where(upper, c, recv)])
        d *= 2
    return c


def solution(mesh):
    sub = _sub_mesh(mesh)
    nz, nx, ny, nc = (sub.shape[a] for a in ALL)

    def ar_rep(b):
        return _bfly(_bfly(b, INNER_REP, nc), OUTER_REP, ny)

    def ar_all(b):
        b = _rs(_rs(b, INNER_REP, nc), OUTER_REP, ny)
        b = _bfly(_bfly(b, INNER_ROWS, nx), OUTER_ROWS, nz)
        return _ag(_ag(b, OUTER_REP, ny), INNER_REP, nc)

    def shards(
        grad_shards, error_shards, momentum, weights, q_start, vec_grads, vec_momentum, vec_weights
    ):
        replicas = lax.axis_size(OUTER_REP) * lax.axis_size(INNER_REP)
        first_rep = (lax.axis_index(OUTER_REP) == 0) & (lax.axis_index(INNER_REP) == 0)
        mats, rows, width = grad_shards.shape[1:]
        rank = q_start.shape[2]
        merged = grad_shards[0].astype(jnp.float32) + error_shards[0]
        factor_qt = jnp.swapaxes(q_start, 1, 2)
        vec = vec_grads[0]
        vec_sum = None
        ortho_pt = None
        lanes = 128
        group = lanes * ny * nc
        for repeat in range(ROUNDS):
            local_pt = jnp.einsum("mrd,mkd->mkr", merged, factor_qt, precision=lax.Precision.HIGHEST)
            flat_p = local_pt.reshape(-1)
            if repeat == 0:
                flat = jnp.concatenate([flat_p, vec.reshape(-1)])
                summed = ar_rep(flat.reshape(-1, lanes)).reshape(-1)
                vec_sum = summed[flat_p.size :].reshape(vec.shape)
                summed_pt = summed[: flat_p.size].reshape(local_pt.shape)
            else:
                summed_pt = ar_rep(local_pt.reshape(-1, lanes)).reshape(local_pt.shape)
            local_gram = jnp.einsum("mkr,mlr->mkl", summed_pt, summed_pt, precision=lax.Precision.HIGHEST)
            local_gram = jnp.where(first_rep, local_gram, jnp.zeros_like(local_gram))
            local_qt = jnp.einsum("mrd,mkr->mkd", merged, summed_pt, precision=lax.Precision.HIGHEST)
            pieces = [local_qt.reshape(-1), local_gram.reshape(-1)]
            used = sum(x.size for x in pieces)
            padded = -(-used // group) * group
            pieces.append(jnp.zeros((padded - used,), jnp.float32))
            packed = jnp.concatenate(pieces).reshape(-1, lanes)
            total = ar_all(packed).reshape(-1)
            qt_un = total[: local_qt.size].reshape(local_qt.shape)
            gram_mat = total[local_qt.size : used].reshape(local_gram.shape)
            factor_l = jnp.linalg.cholesky(gram_mat)
            if repeat == ROUNDS - 1:
                rhs = jnp.concatenate([summed_pt, qt_un], axis=2)
                solved = lax.linalg.triangular_solve(factor_l, rhs, left_side=True, lower=True)
                ortho_pt = solved[:, :, :rows]
                factor_qt = solved[:, :, rows:]
            else:
                factor_qt = lax.linalg.triangular_solve(factor_l, qt_un, left_side=True, lower=True)
        low_rank = jnp.einsum(
            "mkr,mkd->mrd", ortho_pt, factor_qt / replicas, precision=lax.Precision.HIGHEST
        )
        new_errors = (merged - low_rank)[None]
        new_momentum = momentum_beta * momentum + low_rank
        new_weights = weights - learn_rate * new_momentum
        vec_mean = vec_sum / replicas
        new_vec_momentum = momentum_beta * vec_momentum + vec_mean
        new_vec_weights = vec_weights - learn_rate * new_vec_momentum
        return (new_errors, new_momentum, new_weights, new_vec_momentum, new_vec_weights)

    rows_axes = (OUTER_ROWS, INNER_ROWS)
    rep_axes = REP
    return jax.shard_map(
        shards,
        mesh=sub,
        in_specs=(
            P(rep_axes, None, rows_axes, None),
            P(rep_axes, None, rows_axes, None),
            P(None, rows_axes, None),
            P(None, rows_axes, None),
            P(),
            P(rep_axes, None, rows_axes),
            P(None, rows_axes),
            P(None, rows_axes),
        ),
        out_specs=(
            P(rep_axes, None, rows_axes, None),
            P(None, rows_axes, None),
            P(None, rows_axes, None),
            P(None, rows_axes),
            P(None, rows_axes),
        ),
        check_vma=False,
    )
```

```python
import jax
import jax.numpy as jnp
import numpy as np
from jax import lax
from jax.experimental import pallas as pl
from jax.experimental.pallas import tpu as pltpu
from jax.sharding import Mesh
from jax.sharding import PartitionSpec as P

ROUNDS = 2

learn_rate = 0.1
momentum_beta = 0.9


OUTER_ROWS, INNER_ROWS, OUTER_REP, INNER_REP = "zr", "xr", "yr", "cr"
ALL = (OUTER_ROWS, INNER_ROWS, OUTER_REP, INNER_REP)
REP = (OUTER_REP, INNER_REP)


def _sub_mesh(mesh):
    rows, rep = mesh.shape["rows"], mesh.shape["rep"]
    devs = np.asarray(mesh.devices)
    xs = []
    for d in devs[:, 0]:
        c = getattr(d, "coords", None)
        if c is None:
            break
        c = tuple(c)
        if xs and c[1:] != xs[0][1:]:
            break
        xs.append(c)
    inner_rows = len(xs) if xs and rows % len(xs) == 0 else 1
    inner_rep = 2 if rep % 2 == 0 else 1
    shape = (rows // inner_rows, inner_rows, rep // inner_rep, inner_rep)
    return Mesh(devs.reshape(shape), ALL)


def _xor(v, axis, d, n):
    return lax.ppermute(v, axis, [(i, i ^ d) for i in range(n)])


def _halves(n):
    d = n // 2
    while d >= 1:
        yield d
        d //= 2


def _bfly(c, axis, n):
    d = 1
    while d < n:
        c = c + _xor(c, axis, d, n)
        d *= 2
    return c


def _rs(b, axis, n):
    k = lax.axis_index(axis)
    for d in _halves(n):
        half = b.shape[0] // 2
        bit = (k // d) % 2
        keep = lax.dynamic_slice_in_dim(b, bit * half, half, 0)
        send = lax.dynamic_slice_in_dim(b, (1 - bit) * half, half, 0)
        b = keep + _xor(send, axis, d, n)
    return b


def _ag(c, axis, n):
    k = lax.axis_index(axis)
    d = 1
    while d < n:
        recv = _xor(c, axis, d, n)
        upper = (k // d) % 2 == 1
        c = jnp.concatenate([jnp.where(upper, recv, c), jnp.where(upper, c, recv)])
        d *= 2
    return c


def _chol_inv_kernel(g_ref, out_ref):
    a = g_ref[...]
    m, n, _ = a.shape
    rows = lax.broadcasted_iota(jnp.int32, (m, n, n), 1)
    cols = lax.broadcasted_iota(jnp.int32, (m, n, n), 2)
    rows_col = lax.broadcasted_iota(jnp.int32, (m, n, 1), 1)
    eye = rows == cols
    y = jnp.where(eye, 1.0, 0.0).astype(jnp.float32)
    for j in range(n):
        c = a[:, :, j : j + 1]
        d = c[:, j : j + 1, :]
        inv_d = 1.0 / jnp.sqrt(d)
        lcol = jnp.where(rows_col >= j, c * inv_d, 0.0)
        lrow = jnp.sum(jnp.where(eye, lcol, 0.0), axis=1, keepdims=True)
        a = a - lcol * lrow
        yj = y[:, j : j + 1, :] * inv_d
        y = jnp.where(rows == j, yj, y - jnp.where(rows_col > j, lcol, 0.0) * yj)
    out_ref[...] = y


def _chol_inv(g):
    m, n, _ = g.shape
    return pl.pallas_call(
        _chol_inv_kernel,
        out_shape=jax.ShapeDtypeStruct(g.shape, jnp.float32),
        in_specs=[pl.BlockSpec(memory_space=pltpu.VMEM)],
        out_specs=pl.BlockSpec(memory_space=pltpu.VMEM),
        cost_estimate=pl.CostEstimate(flops=6 * m * n * n * n, transcendentals=m * n, bytes_accessed=8 * m * n * n),
    )(g)


def solution(mesh):
    sub = _sub_mesh(mesh)
    nz, nx, ny, nc = (sub.shape[a] for a in ALL)

    def ar_rep(b):
        return _bfly(_bfly(b, INNER_REP, nc), OUTER_REP, ny)

    def ar_all(b):
        b = _rs(_rs(b, INNER_REP, nc), OUTER_REP, ny)
        b = _bfly(_bfly(b, INNER_ROWS, nx), OUTER_ROWS, nz)
        return _ag(_ag(b, OUTER_REP, ny), INNER_REP, nc)

    def shards(
        grad_shards, error_shards, momentum, weights, q_start, vec_grads, vec_momentum, vec_weights
    ):
        replicas = lax.axis_size(OUTER_REP) * lax.axis_size(INNER_REP)
        first_rep = (lax.axis_index(OUTER_REP) == 0) & (lax.axis_index(INNER_REP) == 0)
        mats, rows, width = grad_shards.shape[1:]
        rank = q_start.shape[2]
        merged = grad_shards[0].astype(jnp.float32) + error_shards[0]
        factor_qt = jnp.swapaxes(q_start, 1, 2)
        vec = vec_grads[0]
        vec_sum = None
        ortho_pt = None
        lanes = 128
        group = lanes * ny * nc
        for repeat in range(ROUNDS):
            local_pt = jnp.einsum("mrd,mkd->mkr", merged, factor_qt, precision=lax.Precision.HIGHEST)
            flat_p = local_pt.reshape(-1)
            if repeat == 0:
                flat = jnp.concatenate([flat_p, vec.reshape(-1)])
                summed = ar_rep(flat.reshape(-1, lanes)).reshape(-1)
                vec_sum = summed[flat_p.size :].reshape(vec.shape)
                summed_pt = summed[: flat_p.size].reshape(local_pt.shape)
            else:
                summed_pt = ar_rep(local_pt.reshape(-1, lanes)).reshape(local_pt.shape)
            local_gram = jnp.einsum("mkr,mlr->mkl", summed_pt, summed_pt, precision=lax.Precision.HIGHEST)
            local_gram = jnp.where(first_rep, local_gram, jnp.zeros_like(local_gram))
            local_qt = jnp.einsum("mrd,mkr->mkd", merged, summed_pt, precision=lax.Precision.HIGHEST)
            pieces = [local_qt.reshape(-1), local_gram.reshape(-1)]
            used = sum(x.size for x in pieces)
            padded = -(-used // group) * group
            pieces.append(jnp.zeros((padded - used,), jnp.float32))
            packed = jnp.concatenate(pieces).reshape(-1, lanes)
            total = ar_all(packed).reshape(-1)
            qt_un = total[: local_qt.size].reshape(local_qt.shape)
            gram_mat = total[local_qt.size : used].reshape(local_gram.shape)
            inv_l = _chol_inv(gram_mat)
            factor_qt = jnp.einsum("mkl,mld->mkd", inv_l, qt_un, precision=lax.Precision.HIGHEST)
            if repeat == ROUNDS - 1:
                ortho_pt = jnp.einsum("mkl,mlr->mkr", inv_l, summed_pt, precision=lax.Precision.HIGHEST)
        low_rank = jnp.einsum(
            "mkr,mkd->mrd", ortho_pt, factor_qt / replicas, precision=lax.Precision.HIGHEST
        )
        new_errors = (merged - low_rank)[None]
        new_momentum = momentum_beta * momentum + low_rank
        new_weights = weights - learn_rate * new_momentum
        vec_mean = vec_sum / replicas
        new_vec_momentum = momentum_beta * vec_momentum + vec_mean
        new_vec_weights = vec_weights - learn_rate * new_vec_momentum
        return (new_errors, new_momentum, new_weights, new_vec_momentum, new_vec_weights)

    rows_axes = (OUTER_ROWS, INNER_ROWS)
    rep_axes = REP
    return jax.shard_map(
        shards,
        mesh=sub,
        in_specs=(
            P(rep_axes, None, rows_axes, None),
            P(rep_axes, None, rows_axes, None),
            P(None, rows_axes, None),
            P(None, rows_axes, None),
            P(),
            P(rep_axes, None, rows_axes),
            P(None, rows_axes),
            P(None, rows_axes),
        ),
        out_specs=(
            P(rep_axes, None, rows_axes, None),
            P(None, rows_axes, None),
            P(None, rows_axes, None),
            P(None, rows_axes),
            P(None, rows_axes),
        ),
        check_vma=False,
    )
```

```python
import jax
import jax.numpy as jnp
import numpy as np
from jax import lax
from jax.experimental import pallas as pl
from jax.experimental.pallas import tpu as pltpu
from jax.sharding import Mesh
from jax.sharding import PartitionSpec as P

ROUNDS = 2

learn_rate = 0.1
momentum_beta = 0.9


OUTER_ROWS, INNER_ROWS, OUTER_REP, INNER_REP = "zr", "xr", "yr", "cr"
ALL = (OUTER_ROWS, INNER_ROWS, OUTER_REP, INNER_REP)
REP = (OUTER_REP, INNER_REP)


def _sub_mesh(mesh):
    rows, rep = mesh.shape["rows"], mesh.shape["rep"]
    devs = np.asarray(mesh.devices)
    xs = []
    for d in devs[:, 0]:
        c = getattr(d, "coords", None)
        if c is None:
            break
        c = tuple(c)
        if xs and c[1:] != xs[0][1:]:
            break
        xs.append(c)
    inner_rows = len(xs) if xs and rows % len(xs) == 0 else 1
    inner_rep = 2 if rep % 2 == 0 else 1
    shape = (rows // inner_rows, inner_rows, rep // inner_rep, inner_rep)
    return Mesh(devs.reshape(shape), ALL)


def _xor(v, axis, d, n):
    return lax.ppermute(v, axis, [(i, i ^ d) for i in range(n)])


def _halves(n):
    d = n // 2
    while d >= 1:
        yield d
        d //= 2


def _bfly(c, axis, n):
    d = 1
    while d < n:
        c = c + _xor(c, axis, d, n)
        d *= 2
    return c


def _rs(b, axis, n):
    k = lax.axis_index(axis)
    for d in _halves(n):
        half = b.shape[0] // 2
        bit = (k // d) % 2
        keep = lax.dynamic_slice_in_dim(b, bit * half, half, 0)
        send = lax.dynamic_slice_in_dim(b, (1 - bit) * half, half, 0)
        b = keep + _xor(send, axis, d, n)
    return b


def _ag(c, axis, n):
    k = lax.axis_index(axis)
    d = 1
    while d < n:
        recv = _xor(c, axis, d, n)
        upper = (k // d) % 2 == 1
        c = jnp.concatenate([jnp.where(upper, recv, c), jnp.where(upper, c, recv)])
        d *= 2
    return c


def _shift(v, axis, s, n):
    return lax.ppermute(v, axis, [(i, (i + s) % n) for i in range(n)])


def _rs_direct(b, axis, n):
    size = b.shape[0] // n
    k = lax.axis_index(axis)
    acc = lax.dynamic_slice_in_dim(b, k * size, size, 0)
    for s in range(1, n):
        part = lax.dynamic_slice_in_dim(b, ((k + s) % n) * size, size, 0)
        acc = acc + _shift(part, axis, s, n)
    return acc


def _ag_direct(c, axis, n):
    size = c.shape[0]
    k = lax.axis_index(axis)
    out = jnp.zeros((n * size,) + c.shape[1:], c.dtype)
    out = lax.dynamic_update_slice_in_dim(out, c, k * size, 0)
    for s in range(1, n):
        out = lax.dynamic_update_slice_in_dim(out, _shift(c, axis, s, n), ((k - s) % n) * size, 0)
    return out


def _ar_a2a(b, axes, n):
    rows = b.shape[0]
    size = -(-rows // n)
    b = jnp.pad(b, ((0, n * size - rows), (0, 0)))
    parts = lax.all_to_all(b, axes, 0, 0, tiled=True).reshape((n, size) + b.shape[1:])
    mine = jnp.sum(parts, axis=0)
    spread = jnp.broadcast_to(mine[None], (n,) + mine.shape).reshape(b.shape)
    return lax.all_to_all(spread, axes, 0, 0, tiled=True)[:rows]


def _chol_inv_kernel(g_ref, out_ref):
    a = g_ref[...]
    m, n, _ = a.shape
    rows = lax.broadcasted_iota(jnp.int32, (m, n, n), 1)
    cols = lax.broadcasted_iota(jnp.int32, (m, n, n), 2)
    rows_col = lax.broadcasted_iota(jnp.int32, (m, n, 1), 1)
    eye = rows == cols
    y = jnp.where(eye, 1.0, 0.0).astype(jnp.float32)
    for j in range(n):
        c = a[:, :, j : j + 1]
        d = c[:, j : j + 1, :]
        inv_d = 1.0 / jnp.sqrt(d)
        lcol = jnp.where(rows_col >= j, c * inv_d, 0.0)
        lrow = jnp.sum(jnp.where(eye, lcol, 0.0), axis=1, keepdims=True)
        a = a - lcol * lrow
        yj = y[:, j : j + 1, :] * inv_d
        y = jnp.where(rows == j, yj, y - jnp.where(rows_col > j, lcol, 0.0) * yj)
    out_ref[...] = y


def _chol_inv(g):
    m, n, _ = g.shape
    return pl.pallas_call(
        _chol_inv_kernel,
        out_shape=jax.ShapeDtypeStruct(g.shape, jnp.float32),
        in_specs=[pl.BlockSpec(memory_space=pltpu.VMEM)],
        out_specs=pl.BlockSpec(memory_space=pltpu.VMEM),
        cost_estimate=pl.CostEstimate(flops=6 * m * n * n * n, transcendentals=m * n, bytes_accessed=8 * m * n * n),
    )(g)


def solution(mesh):
    sub = _sub_mesh(mesh)
    nz, nx, ny, nc = (sub.shape[a] for a in ALL)

    def ar_rep(b):
        return _bfly(_bfly(b, INNER_REP, nc), OUTER_REP, ny)

    def ar_all(b):
        b = _rs_direct(_rs(b, INNER_REP, nc), OUTER_REP, ny)
        b = _ar_a2a(b, (OUTER_ROWS, INNER_ROWS), nz * nx)
        return _ag(_ag_direct(b, OUTER_REP, ny), INNER_REP, nc)

    def shards(
        grad_shards, error_shards, momentum, weights, q_start, vec_grads, vec_momentum, vec_weights
    ):
        replicas = lax.axis_size(OUTER_REP) * lax.axis_size(INNER_REP)
        first_rep = (lax.axis_index(OUTER_REP) == 0) & (lax.axis_index(INNER_REP) == 0)
        mats, rows, width = grad_shards.shape[1:]
        rank = q_start.shape[2]
        merged = grad_shards[0].astype(jnp.float32) + error_shards[0]
        factor_qt = jnp.swapaxes(q_start, 1, 2)
        vec = vec_grads[0]
        vec_sum = None
        ortho_pt = None
        lanes = 128
        group = lanes * ny * nc
        for repeat in range(ROUNDS):
            local_pt = jnp.einsum("mrd,mkd->mkr", merged, factor_qt, precision=lax.Precision.HIGHEST)
            flat_p = local_pt.reshape(-1)
            if repeat == 0:
                flat = jnp.concatenate([flat_p, vec.reshape(-1)])
                summed = ar_rep(flat.reshape(-1, lanes)).reshape(-1)
                vec_sum = summed[flat_p.size :].reshape(vec.shape)
                summed_pt = summed[: flat_p.size].reshape(local_pt.shape)
            else:
                summed_pt = ar_rep(local_pt.reshape(-1, lanes)).reshape(local_pt.shape)
            local_gram = jnp.einsum("mkr,mlr->mkl", summed_pt, summed_pt, precision=lax.Precision.HIGHEST)
            local_gram = jnp.where(first_rep, local_gram, jnp.zeros_like(local_gram))
            local_qt = jnp.einsum("mrd,mkr->mkd", merged, summed_pt, precision=lax.Precision.HIGHEST)
            pieces = [local_qt.reshape(-1), local_gram.reshape(-1)]
            used = sum(x.size for x in pieces)
            padded = -(-used // group) * group
            pieces.append(jnp.zeros((padded - used,), jnp.float32))
            packed = jnp.concatenate(pieces).reshape(-1, lanes)
            total = ar_all(packed).reshape(-1)
            qt_un = total[: local_qt.size].reshape(local_qt.shape)
            gram_mat = total[local_qt.size : used].reshape(local_gram.shape)
            inv_l = _chol_inv(gram_mat)
            factor_qt = jnp.einsum("mkl,mld->mkd", inv_l, qt_un, precision=lax.Precision.HIGHEST)
            if repeat == ROUNDS - 1:
                ortho_pt = jnp.einsum("mkl,mlr->mkr", inv_l, summed_pt, precision=lax.Precision.HIGHEST)
        low_rank = jnp.einsum(
            "mkr,mkd->mrd", ortho_pt, factor_qt / replicas, precision=lax.Precision.HIGHEST
        )
        new_errors = (merged - low_rank)[None]
        new_momentum = momentum_beta * momentum + low_rank
        new_weights = weights - learn_rate * new_momentum
        vec_mean = vec_sum / replicas
        new_vec_momentum = momentum_beta * vec_momentum + vec_mean
        new_vec_weights = vec_weights - learn_rate * new_vec_momentum
        return (new_errors, new_momentum, new_weights, new_vec_momentum, new_vec_weights)

    rows_axes = (OUTER_ROWS, INNER_ROWS)
    rep_axes = REP
    return jax.shard_map(
        shards,
        mesh=sub,
        in_specs=(
            P(rep_axes, None, rows_axes, None),
            P(rep_axes, None, rows_axes, None),
            P(None, rows_axes, None),
            P(None, rows_axes, None),
            P(),
            P(rep_axes, None, rows_axes),
            P(None, rows_axes),
            P(None, rows_axes),
        ),
        out_specs=(
            P(rep_axes, None, rows_axes, None),
            P(None, rows_axes, None),
            P(None, rows_axes, None),
            P(None, rows_axes),
            P(None, rows_axes),
        ),
        check_vma=False,
    )
```

```python
import jax
import jax.numpy as jnp
import numpy as np
from jax import lax
from jax.experimental import pallas as pl
from jax.experimental.pallas import tpu as pltpu
from jax.sharding import Mesh
from jax.sharding import PartitionSpec as P

ROUNDS = 2

learn_rate = 0.1
momentum_beta = 0.9


OUTER_ROWS, INNER_ROWS, OUTER_REP, INNER_REP = "zr", "xr", "yr", "cr"
ALL = (OUTER_ROWS, INNER_ROWS, OUTER_REP, INNER_REP)
REP = (OUTER_REP, INNER_REP)


def _sub_mesh(mesh):
    rows, rep = mesh.shape["rows"], mesh.shape["rep"]
    devs = np.asarray(mesh.devices)
    xs = []
    for d in devs[:, 0]:
        c = getattr(d, "coords", None)
        if c is None:
            break
        c = tuple(c)
        if xs and c[1:] != xs[0][1:]:
            break
        xs.append(c)
    inner_rows = len(xs) if xs and rows % len(xs) == 0 else 1
    inner_rep = 2 if rep % 2 == 0 else 1
    shape = (rows // inner_rows, inner_rows, rep // inner_rep, inner_rep)
    return Mesh(devs.reshape(shape), ALL)


def _xor(v, axis, d, n):
    return lax.ppermute(v, axis, [(i, i ^ d) for i in range(n)])


def _halves(n):
    d = n // 2
    while d >= 1:
        yield d
        d //= 2


def _bfly(c, axis, n):
    d = 1
    while d < n:
        c = c + _xor(c, axis, d, n)
        d *= 2
    return c


def _rs(b, axis, n):
    k = lax.axis_index(axis)
    for d in _halves(n):
        half = b.shape[0] // 2
        bit = (k // d) % 2
        keep = lax.dynamic_slice_in_dim(b, bit * half, half, 0)
        send = lax.dynamic_slice_in_dim(b, (1 - bit) * half, half, 0)
        b = keep + _xor(send, axis, d, n)
    return b


def _ag(c, axis, n):
    k = lax.axis_index(axis)
    d = 1
    while d < n:
        recv = _xor(c, axis, d, n)
        upper = (k // d) % 2 == 1
        c = jnp.concatenate([jnp.where(upper, recv, c), jnp.where(upper, c, recv)])
        d *= 2
    return c


def _shift(v, axis, s, n):
    return lax.ppermute(v, axis, [(i, (i + s) % n) for i in range(n)])


def _rs_direct(b, axis, n):
    size = b.shape[0] // n
    k = lax.axis_index(axis)
    acc = lax.dynamic_slice_in_dim(b, k * size, size, 0)
    for s in range(1, n):
        part = lax.dynamic_slice_in_dim(b, ((k + s) % n) * size, size, 0)
        acc = acc + _shift(part, axis, s, n)
    return acc


def _ag_direct(c, axis, n):
    k = lax.axis_index(axis)
    got = jnp.stack([c] + [_shift(c, axis, s, n) for s in range(1, n)])
    ordered = jnp.take(got, (k - jnp.arange(n)) % n, axis=0)
    return ordered.reshape((n * c.shape[0],) + c.shape[1:])


def _ar_a2a(b, axes, n):
    rows = b.shape[0]
    size = -(-rows // n)
    b = jnp.pad(b, ((0, n * size - rows), (0, 0)))
    parts = lax.all_to_all(b, axes, 0, 0, tiled=True).reshape((n, size) + b.shape[1:])
    mine = jnp.sum(parts, axis=0)
    spread = jnp.broadcast_to(mine[None], (n,) + mine.shape).reshape(b.shape)
    return lax.all_to_all(spread, axes, 0, 0, tiled=True)[:rows]


def _chol_inv_kernel(g_ref, out_ref):
    a = g_ref[...]
    m, n, _ = a.shape
    rows = lax.broadcasted_iota(jnp.int32, (m, n, n), 1)
    cols = lax.broadcasted_iota(jnp.int32, (m, n, n), 2)
    rows_col = lax.broadcasted_iota(jnp.int32, (m, n, 1), 1)
    eye = rows == cols
    y = jnp.where(eye, 1.0, 0.0).astype(jnp.float32)
    for j in range(n):
        c = a[:, :, j : j + 1]
        d = c[:, j : j + 1, :]
        inv_d = 1.0 / jnp.sqrt(d)
        lcol = jnp.where(rows_col >= j, c * inv_d, 0.0)
        lrow = jnp.sum(jnp.where(eye, lcol, 0.0), axis=1, keepdims=True)
        a = a - lcol * lrow
        yj = y[:, j : j + 1, :] * inv_d
        y = jnp.where(rows == j, yj, y - jnp.where(rows_col > j, lcol, 0.0) * yj)
    out_ref[...] = y


def _chol_inv(g):
    m, n, _ = g.shape
    return pl.pallas_call(
        _chol_inv_kernel,
        out_shape=jax.ShapeDtypeStruct(g.shape, jnp.float32),
        in_specs=[pl.BlockSpec(memory_space=pltpu.VMEM)],
        out_specs=pl.BlockSpec(memory_space=pltpu.VMEM),
        cost_estimate=pl.CostEstimate(flops=6 * m * n * n * n, transcendentals=m * n, bytes_accessed=8 * m * n * n),
    )(g)


def solution(mesh):
    sub = _sub_mesh(mesh)
    nz, nx, ny, nc = (sub.shape[a] for a in ALL)

    def ar_rep(b):
        return _bfly(_bfly(b, INNER_REP, nc), OUTER_REP, ny)

    def ar_all(b):
        b = _rs_direct(_rs(b, INNER_REP, nc), OUTER_REP, ny)
        b = _ar_a2a(b, (OUTER_ROWS, INNER_ROWS), nz * nx)
        return _ag(_ag_direct(b, OUTER_REP, ny), INNER_REP, nc)

    def shards(
        grad_shards, error_shards, momentum, weights, q_start, vec_grads, vec_momentum, vec_weights
    ):
        replicas = lax.axis_size(OUTER_REP) * lax.axis_size(INNER_REP)
        first_rep = (lax.axis_index(OUTER_REP) == 0) & (lax.axis_index(INNER_REP) == 0)
        mats, rows, width = grad_shards.shape[1:]
        rank = q_start.shape[2]
        merged = grad_shards[0].astype(jnp.float32) + error_shards[0]
        factor_qt = jnp.swapaxes(q_start, 1, 2)
        vec = vec_grads[0]
        vec_sum = None
        ortho_pt = None
        lanes = 128
        group = lanes * ny * nc
        for repeat in range(ROUNDS):
            local_pt = jnp.einsum("mrd,mkd->mkr", merged, factor_qt, precision=lax.Precision.HIGHEST)
            flat_p = local_pt.reshape(-1)
            if repeat == 0:
                flat = jnp.concatenate([flat_p, vec.reshape(-1)])
                summed = ar_rep(flat.reshape(-1, lanes)).reshape(-1)
                vec_sum = summed[flat_p.size :].reshape(vec.shape)
                summed_pt = summed[: flat_p.size].reshape(local_pt.shape)
            else:
                summed_pt = ar_rep(local_pt.reshape(-1, lanes)).reshape(local_pt.shape)
            local_gram = jnp.einsum("mkr,mlr->mkl", summed_pt, summed_pt, precision=lax.Precision.HIGHEST)
            local_gram = jnp.where(first_rep, local_gram, jnp.zeros_like(local_gram))
            local_qt = jnp.einsum("mrd,mkr->mkd", merged, summed_pt, precision=lax.Precision.HIGHEST)
            pieces = [local_qt.reshape(-1), local_gram.reshape(-1)]
            used = sum(x.size for x in pieces)
            padded = -(-used // group) * group
            pieces.append(jnp.zeros((padded - used,), jnp.float32))
            packed = jnp.concatenate(pieces).reshape(-1, lanes)
            total = ar_all(packed).reshape(-1)
            qt_un = total[: local_qt.size].reshape(local_qt.shape)
            gram_mat = total[local_qt.size : used].reshape(local_gram.shape)
            inv_l = _chol_inv(gram_mat)
            factor_qt = jnp.einsum("mkl,mld->mkd", inv_l, qt_un, precision=lax.Precision.HIGHEST)
            if repeat == ROUNDS - 1:
                ortho_pt = jnp.einsum("mkl,mlr->mkr", inv_l, summed_pt, precision=lax.Precision.HIGHEST)
        low_rank = jnp.einsum(
            "mkr,mkd->mrd", ortho_pt, factor_qt / replicas, precision=lax.Precision.HIGHEST
        )
        new_errors = (merged - low_rank)[None]
        new_momentum = momentum_beta * momentum + low_rank
        new_weights = weights - learn_rate * new_momentum
        vec_mean = vec_sum / replicas
        new_vec_momentum = momentum_beta * vec_momentum + vec_mean
        new_vec_weights = vec_weights - learn_rate * new_vec_momentum
        return (new_errors, new_momentum, new_weights, new_vec_momentum, new_vec_weights)

    rows_axes = (OUTER_ROWS, INNER_ROWS)
    rep_axes = REP
    return jax.shard_map(
        shards,
        mesh=sub,
        in_specs=(
            P(rep_axes, None, rows_axes, None),
            P(rep_axes, None, rows_axes, None),
            P(None, rows_axes, None),
            P(None, rows_axes, None),
            P(),
            P(rep_axes, None, rows_axes),
            P(None, rows_axes),
            P(None, rows_axes),
        ),
        out_specs=(
            P(rep_axes, None, rows_axes, None),
            P(None, rows_axes, None),
            P(None, rows_axes, None),
            P(None, rows_axes),
            P(None, rows_axes),
        ),
        check_vma=False,
    )
```

```python
import jax
import jax.numpy as jnp
import numpy as np
from jax import lax
from jax.experimental import pallas as pl
from jax.experimental.pallas import tpu as pltpu
from jax.sharding import Mesh
from jax.sharding import PartitionSpec as P

ROUNDS = 2

learn_rate = 0.1
momentum_beta = 0.9


OUTER_ROWS, INNER_ROWS, OUTER_REP, INNER_REP = "zr", "xr", "yr", "cr"
ALL = (OUTER_ROWS, INNER_ROWS, OUTER_REP, INNER_REP)
REP = (OUTER_REP, INNER_REP)


def _sub_mesh(mesh):
    rows, rep = mesh.shape["rows"], mesh.shape["rep"]
    devs = np.asarray(mesh.devices)
    xs = []
    for d in devs[:, 0]:
        c = getattr(d, "coords", None)
        if c is None:
            break
        c = tuple(c)
        if xs and c[1:] != xs[0][1:]:
            break
        xs.append(c)
    inner_rows = len(xs) if xs and rows % len(xs) == 0 else 1
    inner_rep = 2 if rep % 2 == 0 else 1
    shape = (rows // inner_rows, inner_rows, rep // inner_rep, inner_rep)
    return Mesh(devs.reshape(shape), ALL)


def _xor(v, axis, d, n):
    return lax.ppermute(v, axis, [(i, i ^ d) for i in range(n)])


def _halves(n):
    d = n // 2
    while d >= 1:
        yield d
        d //= 2


def _bfly(c, axis, n):
    d = 1
    while d < n:
        c = c + _xor(c, axis, d, n)
        d *= 2
    return c


def _rs(b, axis, n):
    k = lax.axis_index(axis)
    for d in _halves(n):
        half = b.shape[0] // 2
        bit = (k // d) % 2
        keep = lax.dynamic_slice_in_dim(b, bit * half, half, 0)
        send = lax.dynamic_slice_in_dim(b, (1 - bit) * half, half, 0)
        b = keep + _xor(send, axis, d, n)
    return b


def _ag(c, axis, n):
    k = lax.axis_index(axis)
    d = 1
    while d < n:
        recv = _xor(c, axis, d, n)
        upper = (k // d) % 2 == 1
        c = jnp.concatenate([jnp.where(upper, recv, c), jnp.where(upper, c, recv)])
        d *= 2
    return c


def _shift(v, axis, s, n):
    return lax.ppermute(v, axis, [(i, (i + s) % n) for i in range(n)])


def _rs_direct(b, axis, n):
    size = b.shape[0] // n
    k = lax.axis_index(axis)
    acc = lax.dynamic_slice_in_dim(b, k * size, size, 0)
    for s in range(1, n):
        part = lax.dynamic_slice_in_dim(b, ((k + s) % n) * size, size, 0)
        acc = acc + _shift(part, axis, s, n)
    return acc


def _ag_direct(c, axis, n):
    k = lax.axis_index(axis)
    got = jnp.stack([c] + [_shift(c, axis, s, n) for s in range(1, n)])
    ordered = jnp.take(got, (k - jnp.arange(n)) % n, axis=0)
    return ordered.reshape((n * c.shape[0],) + c.shape[1:])


def _ar_a2a(b, axes, n):
    rows = b.shape[0]
    size = -(-rows // n)
    b = jnp.pad(b, ((0, n * size - rows), (0, 0)))
    parts = lax.all_to_all(b, axes, 0, 0, tiled=True).reshape((n, size) + b.shape[1:])
    mine = jnp.sum(parts, axis=0)
    spread = jnp.broadcast_to(mine[None], (n,) + mine.shape).reshape(b.shape)
    return lax.all_to_all(spread, axes, 0, 0, tiled=True)[:rows]


def _chol_inv_kernel(g_ref, out_ref):
    a = g_ref[...]
    m, n, _ = a.shape
    rows = lax.broadcasted_iota(jnp.int32, (m, n, n), 1)
    cols = lax.broadcasted_iota(jnp.int32, (m, n, n), 2)
    rows_col = lax.broadcasted_iota(jnp.int32, (m, n, 1), 1)
    eye = rows == cols
    y = jnp.where(eye, 1.0, 0.0).astype(jnp.float32)
    for j in range(n):
        c = a[:, :, j : j + 1]
        d = c[:, j : j + 1, :]
        inv_d = 1.0 / jnp.sqrt(d)
        lcol = jnp.where(rows_col >= j, c * inv_d, 0.0)
        lrow = jnp.sum(jnp.where(eye, lcol, 0.0), axis=1, keepdims=True)
        a = a - lcol * lrow
        yj = y[:, j : j + 1, :] * inv_d
        y = jnp.where(rows == j, yj, y - jnp.where(rows_col > j, lcol, 0.0) * yj)
    out_ref[...] = y


def _chol_inv(g):
    m, n, _ = g.shape
    return pl.pallas_call(
        _chol_inv_kernel,
        out_shape=jax.ShapeDtypeStruct(g.shape, jnp.float32),
        in_specs=[pl.BlockSpec(memory_space=pltpu.VMEM)],
        out_specs=pl.BlockSpec(memory_space=pltpu.VMEM),
        cost_estimate=pl.CostEstimate(flops=6 * m * n * n * n, transcendentals=m * n, bytes_accessed=8 * m * n * n),
    )(g)


def solution(mesh):
    sub = _sub_mesh(mesh)
    nz, nx, ny, nc = (sub.shape[a] for a in ALL)

    def ar_rep(b):
        return _bfly(_bfly(b, INNER_REP, nc), OUTER_REP, ny)

    def ar_all(b):
        b = _rs_direct(_rs(b, INNER_REP, nc), OUTER_REP, ny)
        b = _ar_a2a(b, (OUTER_ROWS, INNER_ROWS), nz * nx)
        return _ag(_ag_direct(b, OUTER_REP, ny), INNER_REP, nc)

    def shards(
        grad_shards, error_shards, momentum, weights, q_start, vec_grads, vec_momentum, vec_weights
    ):
        replicas = lax.axis_size(OUTER_REP) * lax.axis_size(INNER_REP)
        first_rep = (lax.axis_index(OUTER_REP) == 0) & (lax.axis_index(INNER_REP) == 0)
        mats, rows, width = grad_shards.shape[1:]
        rank = q_start.shape[2]
        merged = grad_shards[0].astype(jnp.float32) + error_shards[0]
        factor_qt = jnp.swapaxes(q_start, 1, 2)
        vec = vec_grads[0]
        vec_sum = None
        ortho_pt = None
        lanes = 128
        group = lanes * ny * nc
        for repeat in range(ROUNDS):
            local_pt = jnp.einsum("mrd,mkd->mkr", merged, factor_qt, precision=lax.Precision.HIGHEST)
            flat_p = local_pt.reshape(-1)
            if repeat == 0:
                flat = jnp.concatenate([flat_p, vec.reshape(-1)])
                summed = ar_rep(flat.reshape(-1, lanes)).reshape(-1)
                vec_sum = summed[flat_p.size :].reshape(vec.shape)
                summed_pt = summed[: flat_p.size].reshape(local_pt.shape)
            else:
                summed_pt = ar_rep(local_pt.reshape(-1, lanes)).reshape(local_pt.shape)
            local_gram = jnp.einsum("mkr,mlr->mkl", summed_pt, summed_pt, precision=lax.Precision.HIGHEST)
            local_gram = jnp.where(first_rep, local_gram, jnp.zeros_like(local_gram))
            local_qt = jnp.einsum("mrd,mkr->mkd", merged, summed_pt, precision=lax.Precision.HIGHEST)
            tiles = (mats * rank // 8, 8, width // lanes, lanes)
            q_rows = jnp.swapaxes(local_qt.reshape(tiles), 1, 2).reshape(-1, lanes)
            g_rows = local_gram.reshape(-1, lanes)
            used = q_rows.shape[0] + g_rows.shape[0]
            padded = -(-used * lanes // group) * group // lanes
            packed = jnp.concatenate([q_rows, g_rows, jnp.zeros((padded - used, lanes), jnp.float32)])
            total = ar_all(packed)
            qt_un = jnp.swapaxes(total[: q_rows.shape[0]].reshape(tiles[0], tiles[2], 8, lanes), 1, 2).reshape(local_qt.shape)
            gram_mat = total[q_rows.shape[0] : used].reshape(local_gram.shape)
            inv_l = _chol_inv(gram_mat)
            factor_qt = jnp.einsum("mkl,mld->mkd", inv_l, qt_un, precision=lax.Precision.HIGHEST)
            if repeat == ROUNDS - 1:
                ortho_pt = jnp.einsum("mkl,mlr->mkr", inv_l, summed_pt, precision=lax.Precision.HIGHEST)
        low_rank = jnp.einsum(
            "mkr,mkd->mrd", ortho_pt, factor_qt / replicas, precision=lax.Precision.HIGHEST
        )
        new_errors = (merged - low_rank)[None]
        new_momentum = momentum_beta * momentum + low_rank
        new_weights = weights - learn_rate * new_momentum
        vec_mean = vec_sum / replicas
        new_vec_momentum = momentum_beta * vec_momentum + vec_mean
        new_vec_weights = vec_weights - learn_rate * new_vec_momentum
        return (new_errors, new_momentum, new_weights, new_vec_momentum, new_vec_weights)

    rows_axes = (OUTER_ROWS, INNER_ROWS)
    rep_axes = REP
    return jax.shard_map(
        shards,
        mesh=sub,
        in_specs=(
            P(rep_axes, None, rows_axes, None),
            P(rep_axes, None, rows_axes, None),
            P(None, rows_axes, None),
            P(None, rows_axes, None),
            P(),
            P(rep_axes, None, rows_axes),
            P(None, rows_axes),
            P(None, rows_axes),
        ),
        out_specs=(
            P(rep_axes, None, rows_axes, None),
            P(None, rows_axes, None),
            P(None, rows_axes, None),
            P(None, rows_axes),
            P(None, rows_axes),
        ),
        check_vma=False,
    )
```

```python
import jax
import jax.numpy as jnp
import numpy as np
from jax import lax
from jax.experimental import pallas as pl
from jax.experimental.pallas import tpu as pltpu
from jax.sharding import Mesh
from jax.sharding import PartitionSpec as P

ROUNDS = 2

learn_rate = 0.1
momentum_beta = 0.9


OUTER_ROWS, INNER_ROWS, OUTER_REP, INNER_REP = "zr", "xr", "yr", "cr"
ALL = (OUTER_ROWS, INNER_ROWS, OUTER_REP, INNER_REP)
REP = (OUTER_REP, INNER_REP)


def _sub_mesh(mesh):
    rows, rep = mesh.shape["rows"], mesh.shape["rep"]
    devs = np.asarray(mesh.devices)
    xs = []
    for d in devs[:, 0]:
        c = getattr(d, "coords", None)
        if c is None:
            break
        c = tuple(c)
        if xs and c[1:] != xs[0][1:]:
            break
        xs.append(c)
    inner_rows = len(xs) if xs and rows % len(xs) == 0 else 1
    inner_rep = 2 if rep % 2 == 0 else 1
    shape = (rows // inner_rows, inner_rows, rep // inner_rep, inner_rep)
    return Mesh(devs.reshape(shape), ALL)


def _xor(v, axis, d, n):
    return lax.ppermute(v, axis, [(i, i ^ d) for i in range(n)])


def _halves(n):
    d = n // 2
    while d >= 1:
        yield d
        d //= 2


def _bfly(c, axis, n):
    d = 1
    while d < n:
        c = c + _xor(c, axis, d, n)
        d *= 2
    return c


def _rs(b, axis, n):
    k = lax.axis_index(axis)
    for d in _halves(n):
        half = b.shape[0] // 2
        bit = (k // d) % 2
        keep = lax.dynamic_slice_in_dim(b, bit * half, half, 0)
        send = lax.dynamic_slice_in_dim(b, (1 - bit) * half, half, 0)
        b = keep + _xor(send, axis, d, n)
    return b


def _ag(c, axis, n):
    k = lax.axis_index(axis)
    d = 1
    while d < n:
        recv = _xor(c, axis, d, n)
        upper = (k // d) % 2 == 1
        c = jnp.concatenate([jnp.where(upper, recv, c), jnp.where(upper, c, recv)])
        d *= 2
    return c


def _shift(v, axis, s, n):
    return lax.ppermute(v, axis, [(i, (i + s) % n) for i in range(n)])


def _rs_direct(b, axis, n):
    size = b.shape[0] // n
    k = lax.axis_index(axis)
    acc = lax.dynamic_slice_in_dim(b, k * size, size, 0)
    for s in range(1, n):
        part = lax.dynamic_slice_in_dim(b, ((k + s) % n) * size, size, 0)
        acc = acc + _shift(part, axis, s, n)
    return acc


def _ag_direct(c, axis, n):
    k = lax.axis_index(axis)
    got = jnp.stack([c] + [_shift(c, axis, s, n) for s in range(1, n)])
    ordered = jnp.take(got, (k - jnp.arange(n)) % n, axis=0)
    return ordered.reshape((n * c.shape[0],) + c.shape[1:])


def _ar_a2a(b, axes, n):
    rows = b.shape[0]
    size = -(-rows // n)
    b = jnp.pad(b, ((0, n * size - rows), (0, 0)))
    parts = lax.all_to_all(b, axes, 0, 0, tiled=True).reshape((n, size) + b.shape[1:])
    mine = jnp.sum(parts, axis=0)
    spread = jnp.broadcast_to(mine[None], (n,) + mine.shape).reshape(b.shape)
    return lax.all_to_all(spread, axes, 0, 0, tiled=True)[:rows]


def _chol_inv_kernel(g_ref, out_ref):
    a = g_ref[...]
    m, n, _ = a.shape
    rows = lax.broadcasted_iota(jnp.int32, (m, n, n), 1)
    cols = lax.broadcasted_iota(jnp.int32, (m, n, n), 2)
    rows_col = lax.broadcasted_iota(jnp.int32, (m, n, 1), 1)
    eye = rows == cols
    y = jnp.where(eye, 1.0, 0.0).astype(jnp.float32)
    for j in range(n):
        c = a[:, :, j : j + 1]
        d = c[:, j : j + 1, :]
        inv_d = 1.0 / jnp.sqrt(d)
        lcol = jnp.where(rows_col >= j, c * inv_d, 0.0)
        lrow = jnp.sum(jnp.where(eye, lcol, 0.0), axis=1, keepdims=True)
        a = a - lcol * lrow
        yj = y[:, j : j + 1, :] * inv_d
        y = jnp.where(rows == j, yj, y - jnp.where(rows_col > j, lcol, 0.0) * yj)
    out_ref[...] = y


def _chol_inv(g):
    m, n, _ = g.shape
    return pl.pallas_call(
        _chol_inv_kernel,
        out_shape=jax.ShapeDtypeStruct(g.shape, jnp.float32),
        in_specs=[pl.BlockSpec(memory_space=pltpu.VMEM)],
        out_specs=pl.BlockSpec(memory_space=pltpu.VMEM),
        cost_estimate=pl.CostEstimate(flops=6 * m * n * n * n, transcendentals=m * n, bytes_accessed=8 * m * n * n),
    )(g)


def solution(mesh):
    sub = _sub_mesh(mesh)
    nz, nx, ny, nc = (sub.shape[a] for a in ALL)

    def ar_rep(b):
        return _bfly(_bfly(b, INNER_REP, nc), OUTER_REP, ny)

    def ar_all(b):
        b = _rs(b, INNER_REP, nc)
        b = _ar_a2a(b, (OUTER_ROWS, INNER_ROWS, OUTER_REP), nz * nx * ny)
        return _ag(b, INNER_REP, nc)

    def shards(
        grad_shards, error_shards, momentum, weights, q_start, vec_grads, vec_momentum, vec_weights
    ):
        replicas = lax.axis_size(OUTER_REP) * lax.axis_size(INNER_REP)
        first_rep = (lax.axis_index(OUTER_REP) == 0) & (lax.axis_index(INNER_REP) == 0)
        mats, rows, width = grad_shards.shape[1:]
        rank = q_start.shape[2]
        merged = grad_shards[0].astype(jnp.float32) + error_shards[0]
        factor_qt = jnp.swapaxes(q_start, 1, 2)
        vec = vec_grads[0]
        vec_sum = None
        ortho_pt = None
        lanes = 128
        group = lanes * nc
        for repeat in range(ROUNDS):
            local_pt = jnp.einsum("mrd,mkd->mkr", merged, factor_qt, precision=lax.Precision.HIGHEST)
            flat_p = local_pt.reshape(-1)
            if repeat == 0:
                flat = jnp.concatenate([flat_p, vec.reshape(-1)])
                summed = ar_rep(flat.reshape(-1, lanes)).reshape(-1)
                vec_sum = summed[flat_p.size :].reshape(vec.shape)
                summed_pt = summed[: flat_p.size].reshape(local_pt.shape)
            else:
                summed_pt = ar_rep(local_pt.reshape(-1, lanes)).reshape(local_pt.shape)
            local_gram = jnp.einsum("mkr,mlr->mkl", summed_pt, summed_pt, precision=lax.Precision.HIGHEST)
            local_gram = jnp.where(first_rep, local_gram, jnp.zeros_like(local_gram))
            local_qt = jnp.einsum("mrd,mkr->mkd", merged, summed_pt, precision=lax.Precision.HIGHEST)
            tiles = (mats * rank // 8, 8, width // lanes, lanes)
            q_rows = jnp.swapaxes(local_qt.reshape(tiles), 1, 2).reshape(-1, lanes)
            g_rows = local_gram.reshape(-1, lanes)
            used = q_rows.shape[0] + g_rows.shape[0]
            padded = -(-used * lanes // group) * group // lanes
            packed = jnp.concatenate([q_rows, g_rows, jnp.zeros((padded - used, lanes), jnp.float32)])
            total = ar_all(packed)
            qt_un = jnp.swapaxes(total[: q_rows.shape[0]].reshape(tiles[0], tiles[2], 8, lanes), 1, 2).reshape(local_qt.shape)
            gram_mat = total[q_rows.shape[0] : used].reshape(local_gram.shape)
            inv_l = _chol_inv(gram_mat)
            factor_qt = jnp.einsum("mkl,mld->mkd", inv_l, qt_un, precision=lax.Precision.HIGHEST)
            if repeat == ROUNDS - 1:
                ortho_pt = jnp.einsum("mkl,mlr->mkr", inv_l, summed_pt, precision=lax.Precision.HIGHEST)
        low_rank = jnp.einsum(
            "mkr,mkd->mrd", ortho_pt, factor_qt / replicas, precision=lax.Precision.HIGHEST
        )
        new_errors = (merged - low_rank)[None]
        new_momentum = momentum_beta * momentum + low_rank
        new_weights = weights - learn_rate * new_momentum
        vec_mean = vec_sum / replicas
        new_vec_momentum = momentum_beta * vec_momentum + vec_mean
        new_vec_weights = vec_weights - learn_rate * new_vec_momentum
        return (new_errors, new_momentum, new_weights, new_vec_momentum, new_vec_weights)

    rows_axes = (OUTER_ROWS, INNER_ROWS)
    rep_axes = REP
    return jax.shard_map(
        shards,
        mesh=sub,
        in_specs=(
            P(rep_axes, None, rows_axes, None),
            P(rep_axes, None, rows_axes, None),
            P(None, rows_axes, None),
            P(None, rows_axes, None),
            P(),
            P(rep_axes, None, rows_axes),
            P(None, rows_axes),
            P(None, rows_axes),
        ),
        out_specs=(
            P(rep_axes, None, rows_axes, None),
            P(None, rows_axes, None),
            P(None, rows_axes, None),
            P(None, rows_axes),
            P(None, rows_axes),
        ),
        check_vma=False,
    )
```

```python
import jax
import jax.numpy as jnp
import numpy as np
from jax import lax
from jax.experimental import pallas as pl
from jax.experimental.pallas import tpu as pltpu
from jax.sharding import Mesh
from jax.sharding import PartitionSpec as P

ROUNDS = 2

learn_rate = 0.1
momentum_beta = 0.9


OUTER_ROWS, INNER_ROWS, OUTER_REP, INNER_REP = "zr", "xr", "yr", "cr"
ALL = (OUTER_ROWS, INNER_ROWS, OUTER_REP, INNER_REP)
REP = (OUTER_REP, INNER_REP)


def _sub_mesh(mesh):
    rows, rep = mesh.shape["rows"], mesh.shape["rep"]
    devs = np.asarray(mesh.devices)
    xs = []
    for d in devs[:, 0]:
        c = getattr(d, "coords", None)
        if c is None:
            break
        c = tuple(c)
        if xs and c[1:] != xs[0][1:]:
            break
        xs.append(c)
    inner_rows = len(xs) if xs and rows % len(xs) == 0 else 1
    inner_rep = 2 if rep % 2 == 0 else 1
    shape = (rows // inner_rows, inner_rows, rep // inner_rep, inner_rep)
    return Mesh(devs.reshape(shape), ALL)


def _xor(v, axis, d, n):
    return lax.ppermute(v, axis, [(i, i ^ d) for i in range(n)])


def _halves(n):
    d = n // 2
    while d >= 1:
        yield d
        d //= 2


def _bfly(c, axis, n):
    d = 1
    while d < n:
        c = c + _xor(c, axis, d, n)
        d *= 2
    return c


def _rs(b, axis, n):
    k = lax.axis_index(axis)
    for d in _halves(n):
        half = b.shape[0] // 2
        bit = (k // d) % 2
        keep = lax.dynamic_slice_in_dim(b, bit * half, half, 0)
        send = lax.dynamic_slice_in_dim(b, (1 - bit) * half, half, 0)
        b = keep + _xor(send, axis, d, n)
    return b


def _ag(c, axis, n):
    k = lax.axis_index(axis)
    d = 1
    while d < n:
        recv = _xor(c, axis, d, n)
        upper = (k // d) % 2 == 1
        c = jnp.concatenate([jnp.where(upper, recv, c), jnp.where(upper, c, recv)])
        d *= 2
    return c


def _shift(v, axis, s, n):
    return lax.ppermute(v, axis, [(i, (i + s) % n) for i in range(n)])


def _rs_direct(b, axis, n):
    size = b.shape[0] // n
    k = lax.axis_index(axis)
    acc = lax.dynamic_slice_in_dim(b, k * size, size, 0)
    for s in range(1, n):
        part = lax.dynamic_slice_in_dim(b, ((k + s) % n) * size, size, 0)
        acc = acc + _shift(part, axis, s, n)
    return acc


def _ag_direct(c, axis, n):
    k = lax.axis_index(axis)
    got = jnp.stack([c] + [_shift(c, axis, s, n) for s in range(1, n)])
    ordered = jnp.take(got, (k - jnp.arange(n)) % n, axis=0)
    return ordered.reshape((n * c.shape[0],) + c.shape[1:])


def _ar_a2a(b, axes, n):
    rows = b.shape[0]
    size = -(-rows // n)
    b = jnp.pad(b, ((0, n * size - rows), (0, 0)))
    parts = lax.all_to_all(b, axes, 0, 0, tiled=True).reshape((n, size) + b.shape[1:])
    mine = jnp.sum(parts, axis=0)
    spread = jnp.broadcast_to(mine[None], (n,) + mine.shape).reshape(b.shape)
    return lax.all_to_all(spread, axes, 0, 0, tiled=True)[:rows]


def _chol_inv_kernel(g_ref, out_ref):
    a = g_ref[...]
    m, n, _ = a.shape
    rows = lax.broadcasted_iota(jnp.int32, (m, n, n), 1)
    cols = lax.broadcasted_iota(jnp.int32, (m, n, n), 2)
    rows_col = lax.broadcasted_iota(jnp.int32, (m, n, 1), 1)
    eye = rows == cols
    y = jnp.where(eye, 1.0, 0.0).astype(jnp.float32)
    for j in range(n):
        c = a[:, :, j : j + 1]
        d = c[:, j : j + 1, :]
        inv_d = 1.0 / jnp.sqrt(d)
        lcol = jnp.where(rows_col >= j, c * inv_d, 0.0)
        lrow = jnp.sum(jnp.where(eye, lcol, 0.0), axis=1, keepdims=True)
        a = a - lcol * lrow
        yj = y[:, j : j + 1, :] * inv_d
        y = jnp.where(rows == j, yj, y - jnp.where(rows_col > j, lcol, 0.0) * yj)
    out_ref[...] = y


def _chol_inv(g):
    m, n, _ = g.shape
    return pl.pallas_call(
        _chol_inv_kernel,
        out_shape=jax.ShapeDtypeStruct(g.shape, jnp.float32),
        in_specs=[pl.BlockSpec(memory_space=pltpu.VMEM)],
        out_specs=pl.BlockSpec(memory_space=pltpu.VMEM),
        cost_estimate=pl.CostEstimate(flops=6 * m * n * n * n, transcendentals=m * n, bytes_accessed=8 * m * n * n),
    )(g)


def solution(mesh):
    sub = _sub_mesh(mesh)
    nz, nx, ny, nc = (sub.shape[a] for a in ALL)

    def ar_rep(b):
        return _bfly(_bfly(b, INNER_REP, nc), OUTER_REP, ny)

    def ar_all(b):
        b = _rs_direct(_rs(b, INNER_REP, nc), OUTER_REP, ny)
        b = _ar_a2a(b, (OUTER_ROWS, INNER_ROWS), nz * nx)
        return _ag(_ag_direct(b, OUTER_REP, ny), INNER_REP, nc)

    def shards(
        grad_shards, error_shards, momentum, weights, q_start, vec_grads, vec_momentum, vec_weights
    ):
        replicas = lax.axis_size(OUTER_REP) * lax.axis_size(INNER_REP)
        first_rep = (lax.axis_index(OUTER_REP) == 0) & (lax.axis_index(INNER_REP) == 0)
        mats, rows, width = grad_shards.shape[1:]
        rank = q_start.shape[2]
        merged = grad_shards[0].astype(jnp.float32) + error_shards[0]
        factor_qt = jnp.swapaxes(q_start, 1, 2)
        vec = vec_grads[0]
        vec_sum = None
        ortho_pt = None
        lanes = 128
        group = 8 * lanes * ny * nc
        for repeat in range(ROUNDS):
            local_pt = jnp.einsum("mrd,mkd->mkr", merged, factor_qt, precision=lax.Precision.HIGHEST)
            flat_p = local_pt.reshape(-1)
            if repeat == 0:
                flat = jnp.concatenate([flat_p, vec.reshape(-1)])
                summed = ar_rep(flat.reshape(-1, lanes)).reshape(-1)
                vec_sum = summed[flat_p.size :].reshape(vec.shape)
                summed_pt = summed[: flat_p.size].reshape(local_pt.shape)
            else:
                summed_pt = ar_rep(local_pt.reshape(-1, lanes)).reshape(local_pt.shape)
            local_gram = jnp.einsum("mkr,mlr->mkl", summed_pt, summed_pt, precision=lax.Precision.HIGHEST)
            local_gram = jnp.where(first_rep, local_gram, jnp.zeros_like(local_gram))
            local_qt = jnp.einsum("mrd,mkr->mkd", merged, summed_pt, precision=lax.Precision.HIGHEST)
            tiles = (mats * rank // 8, 8, width // lanes, lanes)
            q_rows = jnp.swapaxes(local_qt.reshape(tiles), 1, 2).reshape(-1, lanes)
            g_rows = local_gram.reshape(-1, lanes)
            used = q_rows.shape[0] + g_rows.shape[0]
            padded = -(-used * lanes // group) * group // lanes
            packed = jnp.concatenate([q_rows, g_rows, jnp.zeros((padded - used, lanes), jnp.float32)])
            total = ar_all(packed)
            qt_un = jnp.swapaxes(total[: q_rows.shape[0]].reshape(tiles[0], tiles[2], 8, lanes), 1, 2).reshape(local_qt.shape)
            gram_mat = total[q_rows.shape[0] : used].reshape(local_gram.shape)
            inv_l = _chol_inv(gram_mat)
            factor_qt = jnp.einsum("mkl,mld->mkd", inv_l, qt_un, precision=lax.Precision.HIGHEST)
            if repeat == ROUNDS - 1:
                ortho_pt = jnp.einsum("mkl,mlr->mkr", inv_l, summed_pt, precision=lax.Precision.HIGHEST)
        low_rank = jnp.einsum(
            "mkr,mkd->mrd", ortho_pt, factor_qt / replicas, precision=lax.Precision.HIGHEST
        )
        new_errors = (merged - low_rank)[None]
        new_momentum = momentum_beta * momentum + low_rank
        new_weights = weights - learn_rate * new_momentum
        vec_mean = vec_sum / replicas
        new_vec_momentum = momentum_beta * vec_momentum + vec_mean
        new_vec_weights = vec_weights - learn_rate * new_vec_momentum
        return (new_errors, new_momentum, new_weights, new_vec_momentum, new_vec_weights)

    rows_axes = (OUTER_ROWS, INNER_ROWS)
    rep_axes = REP
    return jax.shard_map(
        shards,
        mesh=sub,
        in_specs=(
            P(rep_axes, None, rows_axes, None),
            P(rep_axes, None, rows_axes, None),
            P(None, rows_axes, None),
            P(None, rows_axes, None),
            P(),
            P(rep_axes, None, rows_axes),
            P(None, rows_axes),
            P(None, rows_axes),
        ),
        out_specs=(
            P(rep_axes, None, rows_axes, None),
            P(None, rows_axes, None),
            P(None, rows_axes, None),
            P(None, rows_axes),
            P(None, rows_axes),
        ),
        check_vma=False,
    )
```

```python
import jax
import jax.numpy as jnp
import numpy as np
from jax import lax
from jax.experimental import pallas as pl
from jax.experimental.pallas import tpu as pltpu
from jax.sharding import Mesh
from jax.sharding import PartitionSpec as P

ROUNDS = 2

learn_rate = 0.1
momentum_beta = 0.9


OUTER_ROWS, INNER_ROWS, OUTER_REP, INNER_REP = "zr", "xr", "yr", "cr"
ALL = (OUTER_ROWS, INNER_ROWS, OUTER_REP, INNER_REP)
REP = (OUTER_REP, INNER_REP)


def _sub_mesh(mesh):
    rows, rep = mesh.shape["rows"], mesh.shape["rep"]
    devs = np.asarray(mesh.devices)
    xs = []
    for d in devs[:, 0]:
        c = getattr(d, "coords", None)
        if c is None:
            break
        c = tuple(c)
        if xs and c[1:] != xs[0][1:]:
            break
        xs.append(c)
    inner_rows = len(xs) if xs and rows % len(xs) == 0 else 1
    inner_rep = 2 if rep % 2 == 0 else 1
    shape = (rows // inner_rows, inner_rows, rep // inner_rep, inner_rep)
    return Mesh(devs.reshape(shape), ALL)


def _xor(v, axis, d, n):
    return lax.ppermute(v, axis, [(i, i ^ d) for i in range(n)])


def _halves(n):
    d = n // 2
    while d >= 1:
        yield d
        d //= 2


def _bfly(c, axis, n):
    d = 1
    while d < n:
        c = c + _xor(c, axis, d, n)
        d *= 2
    return c


def _rs(b, axis, n):
    k = lax.axis_index(axis)
    for d in _halves(n):
        half = b.shape[0] // 2
        bit = (k // d) % 2
        keep = lax.dynamic_slice_in_dim(b, bit * half, half, 0)
        send = lax.dynamic_slice_in_dim(b, (1 - bit) * half, half, 0)
        b = keep + _xor(send, axis, d, n)
    return b


def _ag(c, axis, n):
    k = lax.axis_index(axis)
    d = 1
    while d < n:
        recv = _xor(c, axis, d, n)
        upper = (k // d) % 2 == 1
        c = jnp.concatenate([jnp.where(upper, recv, c), jnp.where(upper, c, recv)])
        d *= 2
    return c


def _shift(v, axis, s, n):
    return lax.ppermute(v, axis, [(i, (i + s) % n) for i in range(n)])


def _rs_direct(b, axis, n):
    size = b.shape[0] // n
    k = lax.axis_index(axis)
    acc = lax.dynamic_slice_in_dim(b, k * size, size, 0)
    for s in range(1, n):
        part = lax.dynamic_slice_in_dim(b, ((k + s) % n) * size, size, 0)
        acc = acc + _shift(part, axis, s, n)
    return acc


def _ag_direct(c, axis, n):
    k = lax.axis_index(axis)
    got = jnp.stack([c] + [_shift(c, axis, s, n) for s in range(1, n)])
    ordered = jnp.take(got, (k - jnp.arange(n)) % n, axis=0)
    return ordered.reshape((n * c.shape[0],) + c.shape[1:])


def _ar_a2a(b, axes, n):
    rows = b.shape[0]
    size = -(-rows // n)
    b = jnp.pad(b, ((0, n * size - rows), (0, 0)))
    parts = lax.all_to_all(b, axes, 0, 0, tiled=True).reshape((n, size) + b.shape[1:])
    mine = jnp.sum(parts, axis=0)
    spread = jnp.broadcast_to(mine[None], (n,) + mine.shape).reshape(b.shape)
    return lax.all_to_all(spread, axes, 0, 0, tiled=True)[:rows]


def _chol_inv_kernel(g_ref, out_ref):
    a = g_ref[...]
    m, n, _ = a.shape
    rows = lax.broadcasted_iota(jnp.int32, (m, n, n), 1)
    cols = lax.broadcasted_iota(jnp.int32, (m, n, n), 2)
    rows_col = lax.broadcasted_iota(jnp.int32, (m, n, 1), 1)
    eye = rows == cols
    y = jnp.where(eye, 1.0, 0.0).astype(jnp.float32)
    for j in range(n):
        c = a[:, :, j : j + 1]
        d = c[:, j : j + 1, :]
        inv_d = 1.0 / jnp.sqrt(d)
        lcol = jnp.where(rows_col >= j, c * inv_d, 0.0)
        lrow = jnp.sum(jnp.where(eye, lcol, 0.0), axis=1, keepdims=True)
        a = a - lcol * lrow
        yj = y[:, j : j + 1, :] * inv_d
        y = jnp.where(rows == j, yj, y - jnp.where(rows_col > j, lcol, 0.0) * yj)
    out_ref[...] = y


def _chol_inv(g):
    m, n, _ = g.shape
    return pl.pallas_call(
        _chol_inv_kernel,
        out_shape=jax.ShapeDtypeStruct(g.shape, jnp.float32),
        in_specs=[pl.BlockSpec(memory_space=pltpu.VMEM)],
        out_specs=pl.BlockSpec(memory_space=pltpu.VMEM),
        cost_estimate=pl.CostEstimate(flops=6 * m * n * n * n, transcendentals=m * n, bytes_accessed=8 * m * n * n),
    )(g)


def solution(mesh):
    sub = _sub_mesh(mesh)
    nz, nx, ny, nc = (sub.shape[a] for a in ALL)

    def ar_rep(b):
        return _bfly(_bfly(b, INNER_REP, nc), OUTER_REP, ny)

    def ar_all(b):
        b = _rs_direct(_rs(b, INNER_REP, nc), OUTER_REP, ny)
        b = _ar_a2a(b, (OUTER_ROWS, INNER_ROWS), nz * nx)
        return _ag(_ag_direct(b, OUTER_REP, ny), INNER_REP, nc)

    def shards(
        grad_shards, error_shards, momentum, weights, q_start, vec_grads, vec_momentum, vec_weights
    ):
        replicas = lax.axis_size(OUTER_REP) * lax.axis_size(INNER_REP)
        first_rep = (lax.axis_index(OUTER_REP) == 0) & (lax.axis_index(INNER_REP) == 0)
        mats, rows, width = grad_shards.shape[1:]
        rank = q_start.shape[2]
        merged = grad_shards[0].astype(jnp.float32) + error_shards[0]
        factor_qt = jnp.swapaxes(q_start, 1, 2)
        vec = vec_grads[0]
        vec_sum = None
        inv_prev = qt_prev = None
        lanes = 128
        group = lanes * ny * nc
        for repeat in range(ROUNDS):
            if repeat == 0:
                local_pt = jnp.einsum("mrd,mkd->mkr", merged, factor_qt, precision=lax.Precision.HIGHEST)
            else:
                proj = jnp.einsum("mrd,mld->mlr", merged, qt_prev, precision=lax.Precision.HIGHEST)
                local_pt = jnp.einsum("mkl,mlr->mkr", inv_prev, proj, precision=lax.Precision.HIGHEST)
            flat_p = local_pt.reshape(-1)
            if repeat == 0:
                flat = jnp.concatenate([flat_p, vec.reshape(-1)])
                summed = ar_rep(flat.reshape(-1, lanes)).reshape(-1)
                vec_sum = summed[flat_p.size :].reshape(vec.shape)
                summed_pt = summed[: flat_p.size].reshape(local_pt.shape)
            else:
                summed_pt = ar_rep(local_pt.reshape(-1, lanes)).reshape(local_pt.shape)
            local_gram = jnp.einsum("mkr,mlr->mkl", summed_pt, summed_pt, precision=lax.Precision.HIGHEST)
            local_gram = jnp.where(first_rep, local_gram, jnp.zeros_like(local_gram))
            local_qt = jnp.einsum("mrd,mkr->mkd", merged, summed_pt, precision=lax.Precision.HIGHEST)
            tiles = (mats * rank // 8, 8, width // lanes, lanes)
            q_rows = jnp.swapaxes(local_qt.reshape(tiles), 1, 2).reshape(-1, lanes)
            g_rows = local_gram.reshape(-1, lanes)
            used = q_rows.shape[0] + g_rows.shape[0]
            padded = -(-used * lanes // group) * group // lanes
            packed = jnp.concatenate([q_rows, g_rows, jnp.zeros((padded - used, lanes), jnp.float32)])
            total = ar_all(packed)
            qt_un = jnp.swapaxes(total[: q_rows.shape[0]].reshape(tiles[0], tiles[2], 8, lanes), 1, 2).reshape(local_qt.shape)
            gram_mat = total[q_rows.shape[0] : used].reshape(local_gram.shape)
            inv_l = _chol_inv(gram_mat)
            inv_prev, qt_prev = inv_l, qt_un
        inv_gram = jnp.einsum("mka,mkb->mab", inv_prev, inv_prev, precision=lax.Precision.HIGHEST)
        weighted_pt = jnp.einsum("mab,mar->mbr", inv_gram, summed_pt, precision=lax.Precision.HIGHEST)
        low_rank = jnp.einsum(
            "mbr,mbd->mrd", weighted_pt, qt_prev / replicas, precision=lax.Precision.HIGHEST
        )
        new_errors = (merged - low_rank)[None]
        new_momentum = momentum_beta * momentum + low_rank
        new_weights = weights - learn_rate * new_momentum
        vec_mean = vec_sum / replicas
        new_vec_momentum = momentum_beta * vec_momentum + vec_mean
        new_vec_weights = vec_weights - learn_rate * new_vec_momentum
        return (new_errors, new_momentum, new_weights, new_vec_momentum, new_vec_weights)

    rows_axes = (OUTER_ROWS, INNER_ROWS)
    rep_axes = REP
    return jax.shard_map(
        shards,
        mesh=sub,
        in_specs=(
            P(rep_axes, None, rows_axes, None),
            P(rep_axes, None, rows_axes, None),
            P(None, rows_axes, None),
            P(None, rows_axes, None),
            P(),
            P(rep_axes, None, rows_axes),
            P(None, rows_axes),
            P(None, rows_axes),
        ),
        out_specs=(
            P(rep_axes, None, rows_axes, None),
            P(None, rows_axes, None),
            P(None, rows_axes, None),
            P(None, rows_axes),
            P(None, rows_axes),
        ),
        check_vma=False,
    )
```

```python
import jax
import jax.numpy as jnp
import numpy as np
from jax import lax
from jax.experimental import pallas as pl
from jax.experimental.pallas import tpu as pltpu
from jax.sharding import Mesh
from jax.sharding import PartitionSpec as P

ROUNDS = 2

learn_rate = 0.1
momentum_beta = 0.9


OUTER_ROWS, INNER_ROWS, OUTER_REP, INNER_REP = "zr", "xr", "yr", "cr"
ALL = (OUTER_ROWS, INNER_ROWS, OUTER_REP, INNER_REP)
REP = (OUTER_REP, INNER_REP)


def _sub_mesh(mesh):
    rows, rep = mesh.shape["rows"], mesh.shape["rep"]
    devs = np.asarray(mesh.devices)
    xs = []
    for d in devs[:, 0]:
        c = getattr(d, "coords", None)
        if c is None:
            break
        c = tuple(c)
        if xs and c[1:] != xs[0][1:]:
            break
        xs.append(c)
    inner_rows = len(xs) if xs and rows % len(xs) == 0 else 1
    inner_rep = 2 if rep % 2 == 0 else 1
    shape = (rows // inner_rows, inner_rows, rep // inner_rep, inner_rep)
    return Mesh(devs.reshape(shape), ALL)


def _xor(v, axis, d, n):
    return lax.ppermute(v, axis, [(i, i ^ d) for i in range(n)])


def _halves(n):
    d = n // 2
    while d >= 1:
        yield d
        d //= 2


def _bfly(c, axis, n):
    d = 1
    while d < n:
        c = c + _xor(c, axis, d, n)
        d *= 2
    return c


def _rs(b, axis, n):
    k = lax.axis_index(axis)
    for d in _halves(n):
        half = b.shape[0] // 2
        bit = (k // d) % 2
        keep = lax.dynamic_slice_in_dim(b, bit * half, half, 0)
        send = lax.dynamic_slice_in_dim(b, (1 - bit) * half, half, 0)
        b = keep + _xor(send, axis, d, n)
    return b


def _ag(c, axis, n):
    k = lax.axis_index(axis)
    d = 1
    while d < n:
        recv = _xor(c, axis, d, n)
        upper = (k // d) % 2 == 1
        c = jnp.concatenate([jnp.where(upper, recv, c), jnp.where(upper, c, recv)])
        d *= 2
    return c


def _shift(v, axis, s, n):
    return lax.ppermute(v, axis, [(i, (i + s) % n) for i in range(n)])


def _rs_direct(b, axis, n):
    size = b.shape[0] // n
    k = lax.axis_index(axis)
    acc = lax.dynamic_slice_in_dim(b, k * size, size, 0)
    for s in range(1, n):
        part = lax.dynamic_slice_in_dim(b, ((k + s) % n) * size, size, 0)
        acc = acc + _shift(part, axis, s, n)
    return acc


def _ag_direct(c, axis, n):
    k = lax.axis_index(axis)
    got = jnp.stack([c] + [_shift(c, axis, s, n) for s in range(1, n)])
    ordered = jnp.take(got, (k - jnp.arange(n)) % n, axis=0)
    return ordered.reshape((n * c.shape[0],) + c.shape[1:])


def _ar_a2a(b, axes, n):
    rows = b.shape[0]
    size = -(-rows // n)
    b = jnp.pad(b, ((0, n * size - rows), (0, 0)))
    parts = lax.all_to_all(b, axes, 0, 0, tiled=True).reshape((n, size) + b.shape[1:])
    mine = jnp.sum(parts, axis=0)
    spread = jnp.broadcast_to(mine[None], (n,) + mine.shape).reshape(b.shape)
    return lax.all_to_all(spread, axes, 0, 0, tiled=True)[:rows]


def _chol_inv_kernel(g_ref, out_ref):
    a = g_ref[...]
    m, n, _ = a.shape
    rows = lax.broadcasted_iota(jnp.int32, (m, n, n), 1)
    cols = lax.broadcasted_iota(jnp.int32, (m, n, n), 2)
    rows_col = lax.broadcasted_iota(jnp.int32, (m, n, 1), 1)
    eye = rows == cols
    y = jnp.where(eye, 1.0, 0.0).astype(jnp.float32)
    for j in range(n):
        c = a[:, :, j : j + 1]
        d = c[:, j : j + 1, :]
        inv_d = 1.0 / jnp.sqrt(d)
        lcol = jnp.where(rows_col >= j, c * inv_d, 0.0)
        lrow = jnp.where(cols[:, j : j + 1, :] >= j, a[:, j : j + 1, :] * inv_d, 0.0)
        a = a - lcol * lrow
        yj = y[:, j : j + 1, :] * inv_d
        y = jnp.where(rows == j, yj, y - jnp.where(rows_col > j, lcol, 0.0) * yj)
    out_ref[...] = y


def _chol_inv(g):
    m, n, _ = g.shape
    return pl.pallas_call(
        _chol_inv_kernel,
        out_shape=jax.ShapeDtypeStruct(g.shape, jnp.float32),
        in_specs=[pl.BlockSpec(memory_space=pltpu.VMEM)],
        out_specs=pl.BlockSpec(memory_space=pltpu.VMEM),
        cost_estimate=pl.CostEstimate(flops=6 * m * n * n * n, transcendentals=m * n, bytes_accessed=8 * m * n * n),
    )(g)


def solution(mesh):
    sub = _sub_mesh(mesh)
    nz, nx, ny, nc = (sub.shape[a] for a in ALL)

    def ar_rep(b):
        return _bfly(_bfly(b, INNER_REP, nc), OUTER_REP, ny)

    def ar_all(b):
        b = _rs_direct(_rs(b, INNER_REP, nc), OUTER_REP, ny)
        b = _ar_a2a(b, (OUTER_ROWS, INNER_ROWS), nz * nx)
        return _ag(_ag_direct(b, OUTER_REP, ny), INNER_REP, nc)

    def shards(
        grad_shards, error_shards, momentum, weights, q_start, vec_grads, vec_momentum, vec_weights
    ):
        replicas = lax.axis_size(OUTER_REP) * lax.axis_size(INNER_REP)
        first_rep = (lax.axis_index(OUTER_REP) == 0) & (lax.axis_index(INNER_REP) == 0)
        mats, rows, width = grad_shards.shape[1:]
        rank = q_start.shape[2]
        merged = grad_shards[0].astype(jnp.float32) + error_shards[0]
        factor_qt = jnp.swapaxes(q_start, 1, 2)
        vec = vec_grads[0]
        vec_sum = None
        inv_prev = qt_prev = None
        lanes = 128
        group = lanes * ny * nc
        for repeat in range(ROUNDS):
            if repeat == 0:
                local_pt = jnp.einsum("mrd,mkd->mkr", merged, factor_qt, precision=lax.Precision.HIGHEST)
            else:
                proj = jnp.einsum("mrd,mld->mlr", merged, qt_prev, precision=lax.Precision.HIGHEST)
                local_pt = jnp.einsum("mkl,mlr->mkr", inv_prev, proj, precision=lax.Precision.HIGHEST)
            flat_p = local_pt.reshape(-1)
            if repeat == 0:
                flat = jnp.concatenate([flat_p, vec.reshape(-1)])
                summed = ar_rep(flat.reshape(-1, lanes)).reshape(-1)
                vec_sum = summed[flat_p.size :].reshape(vec.shape)
                summed_pt = summed[: flat_p.size].reshape(local_pt.shape)
            else:
                summed_pt = ar_rep(local_pt.reshape(-1, lanes)).reshape(local_pt.shape)
            local_gram = jnp.einsum("mkr,mlr->mkl", summed_pt, summed_pt, precision=lax.Precision.HIGHEST)
            local_gram = jnp.where(first_rep, local_gram, jnp.zeros_like(local_gram))
            local_qt = jnp.einsum("mrd,mkr->mkd", merged, summed_pt, precision=lax.Precision.HIGHEST)
            tiles = (mats * rank // 8, 8, width // lanes, lanes)
            q_rows = jnp.swapaxes(local_qt.reshape(tiles), 1, 2).reshape(-1, lanes)
            g_rows = local_gram.reshape(-1, lanes)
            used = q_rows.shape[0] + g_rows.shape[0]
            padded = -(-used * lanes // group) * group // lanes
            packed = jnp.concatenate([q_rows, g_rows, jnp.zeros((padded - used, lanes), jnp.float32)])
            total = ar_all(packed)
            qt_un = jnp.swapaxes(total[: q_rows.shape[0]].reshape(tiles[0], tiles[2], 8, lanes), 1, 2).reshape(local_qt.shape)
            gram_mat = total[q_rows.shape[0] : used].reshape(local_gram.shape)
            inv_l = _chol_inv(gram_mat)
            inv_prev, qt_prev = inv_l, qt_un
        inv_gram = jnp.einsum("mka,mkb->mab", inv_prev, inv_prev, precision=lax.Precision.HIGHEST)
        weighted_pt = jnp.einsum("mab,mar->mbr", inv_gram, summed_pt, precision=lax.Precision.HIGHEST)
        low_rank = jnp.einsum(
            "mbr,mbd->mrd", weighted_pt, qt_prev / replicas, precision=lax.Precision.HIGHEST
        )
        new_errors = (merged - low_rank)[None]
        new_momentum = momentum_beta * momentum + low_rank
        new_weights = weights - learn_rate * new_momentum
        vec_mean = vec_sum / replicas
        new_vec_momentum = momentum_beta * vec_momentum + vec_mean
        new_vec_weights = vec_weights - learn_rate * new_vec_momentum
        return (new_errors, new_momentum, new_weights, new_vec_momentum, new_vec_weights)

    rows_axes = (OUTER_ROWS, INNER_ROWS)
    rep_axes = REP
    return jax.shard_map(
        shards,
        mesh=sub,
        in_specs=(
            P(rep_axes, None, rows_axes, None),
            P(rep_axes, None, rows_axes, None),
            P(None, rows_axes, None),
            P(None, rows_axes, None),
            P(),
            P(rep_axes, None, rows_axes),
            P(None, rows_axes),
            P(None, rows_axes),
        ),
        out_specs=(
            P(rep_axes, None, rows_axes, None),
            P(None, rows_axes, None),
            P(None, rows_axes, None),
            P(None, rows_axes),
            P(None, rows_axes),
        ),
        check_vma=False,
    )
```

```python
import jax
import jax.numpy as jnp
import numpy as np
from jax import lax
from jax.experimental import pallas as pl
from jax.experimental.pallas import tpu as pltpu
from jax.sharding import Mesh
from jax.sharding import PartitionSpec as P

ROUNDS = 2

learn_rate = 0.1
momentum_beta = 0.9


OUTER_ROWS, INNER_ROWS, OUTER_REP, INNER_REP = "zr", "xr", "yr", "cr"
ALL = (OUTER_ROWS, INNER_ROWS, OUTER_REP, INNER_REP)
REP = (OUTER_REP, INNER_REP)


def _sub_mesh(mesh):
    rows, rep = mesh.shape["rows"], mesh.shape["rep"]
    devs = np.asarray(mesh.devices)
    xs = []
    for d in devs[:, 0]:
        c = getattr(d, "coords", None)
        if c is None:
            break
        c = tuple(c)
        if xs and c[1:] != xs[0][1:]:
            break
        xs.append(c)
    inner_rows = len(xs) if xs and rows % len(xs) == 0 else 1
    inner_rep = 2 if rep % 2 == 0 else 1
    shape = (rows // inner_rows, inner_rows, rep // inner_rep, inner_rep)
    return Mesh(devs.reshape(shape), ALL)


def _xor(v, axis, d, n):
    return lax.ppermute(v, axis, [(i, i ^ d) for i in range(n)])


def _halves(n):
    d = n // 2
    while d >= 1:
        yield d
        d //= 2


def _bfly(c, axis, n):
    d = 1
    while d < n:
        c = c + _xor(c, axis, d, n)
        d *= 2
    return c


def _rs(b, axis, n):
    k = lax.axis_index(axis)
    for d in _halves(n):
        half = b.shape[0] // 2
        bit = (k // d) % 2
        keep = lax.dynamic_slice_in_dim(b, bit * half, half, 0)
        send = lax.dynamic_slice_in_dim(b, (1 - bit) * half, half, 0)
        b = keep + _xor(send, axis, d, n)
    return b


def _ag(c, axis, n):
    k = lax.axis_index(axis)
    d = 1
    while d < n:
        recv = _xor(c, axis, d, n)
        upper = (k // d) % 2 == 1
        c = jnp.concatenate([jnp.where(upper, recv, c), jnp.where(upper, c, recv)])
        d *= 2
    return c


def _shift(v, axis, s, n):
    return lax.ppermute(v, axis, [(i, (i + s) % n) for i in range(n)])


def _rs_direct(b, axis, n):
    size = b.shape[0] // n
    k = lax.axis_index(axis)
    acc = lax.dynamic_slice_in_dim(b, k * size, size, 0)
    for s in range(1, n):
        part = lax.dynamic_slice_in_dim(b, ((k + s) % n) * size, size, 0)
        acc = acc + _shift(part, axis, s, n)
    return acc


def _ag_direct(c, axis, n):
    k = lax.axis_index(axis)
    got = jnp.stack([c] + [_shift(c, axis, s, n) for s in range(1, n)])
    ordered = jnp.take(got, (k - jnp.arange(n)) % n, axis=0)
    return ordered.reshape((n * c.shape[0],) + c.shape[1:])


def _ar_a2a(b, axes, n):
    rows = b.shape[0]
    size = -(-rows // n)
    b = jnp.pad(b, ((0, n * size - rows), (0, 0)))
    parts = lax.all_to_all(b, axes, 0, 0, tiled=True).reshape((n, size) + b.shape[1:])
    mine = jnp.sum(parts, axis=0)
    spread = jnp.broadcast_to(mine[None], (n,) + mine.shape).reshape(b.shape)
    return lax.all_to_all(spread, axes, 0, 0, tiled=True)[:rows]


def _chol_inv_kernel(g_ref, out_ref):
    a = g_ref[...]
    m, n, _ = a.shape
    rows = lax.broadcasted_iota(jnp.int32, (m, n, n), 1)
    cols = lax.broadcasted_iota(jnp.int32, (m, n, n), 2)
    rows_col = lax.broadcasted_iota(jnp.int32, (m, n, 1), 1)
    eye = rows == cols
    y = jnp.where(eye, 1.0, 0.0).astype(jnp.float32)
    for j in range(n):
        c = a[:, :, j : j + 1]
        d = c[:, j : j + 1, :]
        inv_d = 1.0 / jnp.sqrt(d)
        lcol = jnp.where(rows_col >= j, c * inv_d, 0.0)
        lrow = jnp.sum(jnp.where(eye, lcol, 0.0), axis=1, keepdims=True)
        a = a - lcol * lrow
        yj = y[:, j : j + 1, :] * inv_d
        y = jnp.where(rows == j, yj, y - jnp.where(rows_col > j, lcol, 0.0) * yj)
    out_ref[...] = y


def _chol_inv(g):
    m, n, _ = g.shape
    return pl.pallas_call(
        _chol_inv_kernel,
        out_shape=jax.ShapeDtypeStruct(g.shape, jnp.float32),
        in_specs=[pl.BlockSpec(memory_space=pltpu.VMEM)],
        out_specs=pl.BlockSpec(memory_space=pltpu.VMEM),
        cost_estimate=pl.CostEstimate(flops=6 * m * n * n * n, transcendentals=m * n, bytes_accessed=8 * m * n * n),
    )(g)


def solution(mesh):
    sub = _sub_mesh(mesh)
    nz, nx, ny, nc = (sub.shape[a] for a in ALL)

    def ar_rep(b):
        return _bfly(_bfly(b, INNER_REP, nc), OUTER_REP, ny)

    def ar_all(b):
        b = _rs_direct(_rs(b, INNER_REP, nc), OUTER_REP, ny)
        b = _ar_a2a(b, (OUTER_ROWS, INNER_ROWS), nz * nx)
        return _ag(_ag_direct(b, OUTER_REP, ny), INNER_REP, nc)

    def shards(
        grad_shards, error_shards, momentum, weights, q_start, vec_grads, vec_momentum, vec_weights
    ):
        replicas = lax.axis_size(OUTER_REP) * lax.axis_size(INNER_REP)
        first_rep = (lax.axis_index(OUTER_REP) == 0) & (lax.axis_index(INNER_REP) == 0)
        mats, rows, width = grad_shards.shape[1:]
        rank = q_start.shape[2]
        merged = grad_shards[0].astype(jnp.float32) + error_shards[0]
        factor_qt = jnp.swapaxes(q_start, 1, 2)
        vec = vec_grads[0]
        vec_sum = None
        inv_prev = qt_prev = None
        lanes = 128
        group = lanes * ny * nc
        for repeat in range(ROUNDS):
            if repeat == 0:
                local_pt = jnp.einsum("mrd,mkd->mkr", merged, factor_qt, precision=lax.Precision.HIGH)
            else:
                proj = jnp.einsum("mrd,mld->mlr", merged, qt_prev, precision=lax.Precision.HIGH)
                local_pt = jnp.einsum("mkl,mlr->mkr", inv_prev, proj, precision=lax.Precision.HIGHEST)
            flat_p = local_pt.reshape(-1)
            if repeat == 0:
                flat = jnp.concatenate([flat_p, vec.reshape(-1)])
                summed = ar_rep(flat.reshape(-1, lanes)).reshape(-1)
                vec_sum = summed[flat_p.size :].reshape(vec.shape)
                summed_pt = summed[: flat_p.size].reshape(local_pt.shape)
            else:
                summed_pt = ar_rep(local_pt.reshape(-1, lanes)).reshape(local_pt.shape)
            local_gram = jnp.einsum("mkr,mlr->mkl", summed_pt, summed_pt, precision=lax.Precision.HIGHEST)
            local_gram = jnp.where(first_rep, local_gram, jnp.zeros_like(local_gram))
            local_qt = jnp.einsum("mrd,mkr->mkd", merged, summed_pt, precision=lax.Precision.HIGH)
            tiles = (mats * rank // 8, 8, width // lanes, lanes)
            q_rows = jnp.swapaxes(local_qt.reshape(tiles), 1, 2).reshape(-1, lanes)
            g_rows = local_gram.reshape(-1, lanes)
            used = q_rows.shape[0] + g_rows.shape[0]
            padded = -(-used * lanes // group) * group // lanes
            packed = jnp.concatenate([q_rows, g_rows, jnp.zeros((padded - used, lanes), jnp.float32)])
            total = ar_all(packed)
            qt_un = jnp.swapaxes(total[: q_rows.shape[0]].reshape(tiles[0], tiles[2], 8, lanes), 1, 2).reshape(local_qt.shape)
            gram_mat = total[q_rows.shape[0] : used].reshape(local_gram.shape)
            inv_l = _chol_inv(gram_mat)
            inv_prev, qt_prev = inv_l, qt_un
        inv_gram = jnp.einsum("mka,mkb->mab", inv_prev, inv_prev, precision=lax.Precision.HIGHEST)
        weighted_pt = jnp.einsum("mab,mar->mbr", inv_gram, summed_pt, precision=lax.Precision.HIGHEST)
        low_rank = jnp.einsum(
            "mbr,mbd->mrd", weighted_pt, qt_prev / replicas, precision=lax.Precision.HIGHEST
        )
        new_errors = (merged - low_rank)[None]
        new_momentum = momentum_beta * momentum + low_rank
        new_weights = weights - learn_rate * new_momentum
        vec_mean = vec_sum / replicas
        new_vec_momentum = momentum_beta * vec_momentum + vec_mean
        new_vec_weights = vec_weights - learn_rate * new_vec_momentum
        return (new_errors, new_momentum, new_weights, new_vec_momentum, new_vec_weights)

    rows_axes = (OUTER_ROWS, INNER_ROWS)
    rep_axes = REP
    return jax.shard_map(
        shards,
        mesh=sub,
        in_specs=(
            P(rep_axes, None, rows_axes, None),
            P(rep_axes, None, rows_axes, None),
            P(None, rows_axes, None),
            P(None, rows_axes, None),
            P(),
            P(rep_axes, None, rows_axes),
            P(None, rows_axes),
            P(None, rows_axes),
        ),
        out_specs=(
            P(rep_axes, None, rows_axes, None),
            P(None, rows_axes, None),
            P(None, rows_axes, None),
            P(None, rows_axes),
            P(None, rows_axes),
        ),
        check_vma=False,
    )
```

```python
import jax
import jax.numpy as jnp
import numpy as np
from jax import lax
from jax.experimental import pallas as pl
from jax.experimental.pallas import tpu as pltpu
from jax.sharding import Mesh
from jax.sharding import PartitionSpec as P

ROUNDS = 2

learn_rate = 0.1
momentum_beta = 0.9


OUTER_ROWS, INNER_ROWS, OUTER_REP, INNER_REP = "zr", "xr", "yr", "cr"
ALL = (OUTER_ROWS, INNER_ROWS, OUTER_REP, INNER_REP)
REP = (OUTER_REP, INNER_REP)


def _sub_mesh(mesh):
    rows, rep = mesh.shape["rows"], mesh.shape["rep"]
    devs = np.asarray(mesh.devices)
    xs = []
    for d in devs[:, 0]:
        c = getattr(d, "coords", None)
        if c is None:
            break
        c = tuple(c)
        if xs and c[1:] != xs[0][1:]:
            break
        xs.append(c)
    inner_rows = len(xs) if xs and rows % len(xs) == 0 else 1
    inner_rep = 2 if rep % 2 == 0 else 1
    shape = (rows // inner_rows, inner_rows, rep // inner_rep, inner_rep)
    return Mesh(devs.reshape(shape), ALL)


def _xor(v, axis, d, n):
    return lax.ppermute(v, axis, [(i, i ^ d) for i in range(n)])


def _halves(n):
    d = n // 2
    while d >= 1:
        yield d
        d //= 2


def _bfly(c, axis, n):
    d = 1
    while d < n:
        c = c + _xor(c, axis, d, n)
        d *= 2
    return c


def _rs(b, axis, n):
    k = lax.axis_index(axis)
    for d in _halves(n):
        half = b.shape[0] // 2
        bit = (k // d) % 2
        keep = lax.dynamic_slice_in_dim(b, bit * half, half, 0)
        send = lax.dynamic_slice_in_dim(b, (1 - bit) * half, half, 0)
        b = keep + _xor(send, axis, d, n)
    return b


def _ag(c, axis, n):
    k = lax.axis_index(axis)
    d = 1
    while d < n:
        recv = _xor(c, axis, d, n)
        upper = (k // d) % 2 == 1
        c = jnp.concatenate([jnp.where(upper, recv, c), jnp.where(upper, c, recv)])
        d *= 2
    return c


def _shift(v, axis, s, n):
    return lax.ppermute(v, axis, [(i, (i + s) % n) for i in range(n)])


def _rs_direct(b, axis, n):
    size = b.shape[0] // n
    k = lax.axis_index(axis)
    acc = lax.dynamic_slice_in_dim(b, k * size, size, 0)
    for s in range(1, n):
        part = lax.dynamic_slice_in_dim(b, ((k + s) % n) * size, size, 0)
        acc = acc + _shift(part, axis, s, n)
    return acc


def _ag_direct(c, axis, n):
    k = lax.axis_index(axis)
    got = jnp.stack([c] + [_shift(c, axis, s, n) for s in range(1, n)])
    ordered = jnp.take(got, (k - jnp.arange(n)) % n, axis=0)
    return ordered.reshape((n * c.shape[0],) + c.shape[1:])


def _ar_a2a(b, axes, n):
    rows = b.shape[0]
    size = -(-rows // n)
    b = jnp.pad(b, ((0, n * size - rows), (0, 0)))
    parts = lax.all_to_all(b, axes, 0, 0, tiled=True).reshape((n, size) + b.shape[1:])
    mine = jnp.sum(parts, axis=0)
    spread = jnp.broadcast_to(mine[None], (n,) + mine.shape).reshape(b.shape)
    return lax.all_to_all(spread, axes, 0, 0, tiled=True)[:rows]


def _chol_inv_kernel(g_ref, out_ref):
    a = g_ref[...]
    m, n, _ = a.shape
    rows = lax.broadcasted_iota(jnp.int32, (m, n, n), 1)
    cols = lax.broadcasted_iota(jnp.int32, (m, n, n), 2)
    rows_col = lax.broadcasted_iota(jnp.int32, (m, n, 1), 1)
    eye = rows == cols
    y = jnp.where(eye, 1.0, 0.0).astype(jnp.float32)
    for j in range(n):
        c = a[:, :, j : j + 1]
        d = c[:, j : j + 1, :]
        inv_d = 1.0 / jnp.sqrt(d)
        lcol = jnp.where(rows_col >= j, c * inv_d, 0.0)
        lrow = jnp.sum(jnp.where(eye, lcol, 0.0), axis=1, keepdims=True)
        a = a - lcol * lrow
        yj = y[:, j : j + 1, :] * inv_d
        y = jnp.where(rows == j, yj, y - jnp.where(rows_col > j, lcol, 0.0) * yj)
    out_ref[...] = y


def _chol_inv(g):
    m, n, _ = g.shape
    return pl.pallas_call(
        _chol_inv_kernel,
        out_shape=jax.ShapeDtypeStruct(g.shape, jnp.float32),
        in_specs=[pl.BlockSpec(memory_space=pltpu.VMEM)],
        out_specs=pl.BlockSpec(memory_space=pltpu.VMEM),
        cost_estimate=pl.CostEstimate(flops=6 * m * n * n * n, transcendentals=m * n, bytes_accessed=8 * m * n * n),
    )(g)


def solution(mesh):
    sub = _sub_mesh(mesh)
    nz, nx, ny, nc = (sub.shape[a] for a in ALL)

    def ar_rep(b):
        return _bfly(_bfly(b, INNER_REP, nc), OUTER_REP, ny)

    def ar_all(b):
        b = _rs_direct(_rs(b, INNER_REP, nc), OUTER_REP, ny)
        b = _ar_a2a(b, (OUTER_ROWS, INNER_ROWS), nz * nx)
        return _ag(_ag_direct(b, OUTER_REP, ny), INNER_REP, nc)

    def shards(
        grad_shards, error_shards, momentum, weights, q_start, vec_grads, vec_momentum, vec_weights
    ):
        replicas = lax.axis_size(OUTER_REP) * lax.axis_size(INNER_REP)
        first_rep = (lax.axis_index(OUTER_REP) == 0) & (lax.axis_index(INNER_REP) == 0)
        mats, rows, width = grad_shards.shape[1:]
        rank = q_start.shape[2]
        merged = grad_shards[0].astype(jnp.float32) + error_shards[0]
        factor_qt = jnp.swapaxes(q_start, 1, 2)
        vec = vec_grads[0]
        vec_sum = None
        inv_prev = qt_prev = None
        lanes = 128
        group = lanes * ny * nc
        for repeat in range(ROUNDS):
            if repeat == 0:
                local_pt = jnp.einsum("mrd,mkd->mkr", merged, factor_qt, precision=lax.Precision.HIGH)
            else:
                proj = jnp.einsum("mrd,mld->mlr", merged, qt_prev, precision=lax.Precision.HIGH)
                local_pt = jnp.einsum("mkl,mlr->mkr", inv_prev, proj, precision=lax.Precision.HIGHEST)
            flat_p = local_pt.reshape(-1)
            if repeat == 0:
                flat = jnp.concatenate([flat_p, vec.reshape(-1)])
                summed = ar_rep(flat.reshape(-1, lanes)).reshape(-1)
                vec_sum = summed[flat_p.size :].reshape(vec.shape)
                summed_pt = summed[: flat_p.size].reshape(local_pt.shape)
            else:
                summed_pt = ar_rep(local_pt.reshape(-1, lanes)).reshape(local_pt.shape)
            local_gram = jnp.einsum("mkr,mlr->mkl", summed_pt, summed_pt, precision=lax.Precision.HIGHEST)
            local_gram = jnp.where(first_rep, local_gram, jnp.zeros_like(local_gram))
            local_qt = jnp.einsum("mrd,mkr->mkd", merged, summed_pt, precision=lax.Precision.HIGH)
            tiles = (mats * rank // 8, 8, width // lanes, lanes)
            q_rows = jnp.swapaxes(local_qt.reshape(tiles), 1, 2).reshape(-1, lanes)
            g_rows = local_gram.reshape(-1, lanes)
            used = q_rows.shape[0] + g_rows.shape[0]
            padded = -(-used * lanes // group) * group // lanes
            packed = jnp.concatenate([q_rows, g_rows, jnp.zeros((padded - used, lanes), jnp.float32)])
            total = ar_all(packed)
            qt_un = jnp.swapaxes(total[: q_rows.shape[0]].reshape(tiles[0], tiles[2], 8, lanes), 1, 2).reshape(local_qt.shape)
            gram_mat = total[q_rows.shape[0] : used].reshape(local_gram.shape)
            inv_l = _chol_inv(gram_mat)
            inv_prev, qt_prev = inv_l, qt_un
        inv_gram = jnp.einsum("mka,mkb->mab", inv_prev, inv_prev, precision=lax.Precision.HIGHEST)
        weighted_pt = jnp.einsum("mab,mar->mbr", inv_gram, summed_pt, precision=lax.Precision.HIGHEST)
        low_rank = jnp.einsum(
            "mbr,mbd->mrd", weighted_pt, qt_prev / replicas, precision=lax.Precision.HIGH
        )
        new_errors = (merged - low_rank)[None]
        new_momentum = momentum_beta * momentum + low_rank
        new_weights = weights - learn_rate * new_momentum
        vec_mean = vec_sum / replicas
        new_vec_momentum = momentum_beta * vec_momentum + vec_mean
        new_vec_weights = vec_weights - learn_rate * new_vec_momentum
        return (new_errors, new_momentum, new_weights, new_vec_momentum, new_vec_weights)

    rows_axes = (OUTER_ROWS, INNER_ROWS)
    rep_axes = REP
    return jax.shard_map(
        shards,
        mesh=sub,
        in_specs=(
            P(rep_axes, None, rows_axes, None),
            P(rep_axes, None, rows_axes, None),
            P(None, rows_axes, None),
            P(None, rows_axes, None),
            P(),
            P(rep_axes, None, rows_axes),
            P(None, rows_axes),
            P(None, rows_axes),
        ),
        out_specs=(
            P(rep_axes, None, rows_axes, None),
            P(None, rows_axes, None),
            P(None, rows_axes, None),
            P(None, rows_axes),
            P(None, rows_axes),
        ),
        check_vma=False,
    )
```
